512 devices in a mesh: rot: 16 (over x, y), slab: 32 (over z, core).
Axes of the slice: x: 4, y: 4, z: 16, core: 2. Of those that a mesh axis runs over, the one named last changes fastest.
Arguments:
- point_feats: bfloat16 [65536, 96], P('slab'), may hold values from -6 to 6
- owners: int32 [16, 65536], P('rot', 'slab'), may hold values from 0 to 31, as said below
- voxel_ids: int32 [16, 65536], P('rot', 'slab'), may hold values from 0 to 2047, as said below
- active_count: int32 [16, 32], P('rot', 'slab'), may hold values from 4 to 16, as said below
- halo_blocks: int32 [16, 32, 2, 2], P('rot', 'slab'), may hold values from 0 to 15, as said below
- neighbors: int32 [16, 27, 65536], P('rot', None, 'slab'), may hold values from 0 to 2560, as said below
- conv1_weight: bfloat16 [27, 96, 128], replicated, may hold values from -0.125 to 0.125
- conv1_scale: float32 [128], replicated, may hold values from 0.1 to 1.9
- conv1_shift: float32 [128], replicated, may hold values from -3 to 3
- conv2_weight: bfloat16 [27, 128, 128], replicated, may hold values from -0.109375 to 0.109375
- conv2_scale: float32 [128], replicated, may hold values from 0.1 to 1.9
- conv2_shift: float32 [128], replicated, may hold values from -3 to 3
- head_weight: bfloat16 [128, 8], replicated, may hold values from -0.5 to 0.5
- head_bias: float32 [8], replicated, may hold values from -4 to 4
Outputs:
- logits: float32 [8, 65536], P(None, 'slab')
The draws below stay inside these ranges and needn't reach their ends.
Inputs may be any that keep to these rules, and one draw needn't show every extreme that they name: `owners`: in each copy, of the points of one slab at most 192 lie in voxels of any one slab, and one slab receives exactly 192 points from every slab. `voxel_ids`: A point's voxel slot is active in its owner slab: below active_count of that slab times 128. `active_count`: the active blocks of a slab are its first ones; in every copy some slab has all 16 active. `halo_blocks`: every listed block is active in the slab that sends it. `neighbors`: entries index the slab's extended voxel array; row 2560 is the zero row, which all entries of inactive voxels name; offset 13 of an active voxel names itself; rows of own voxels that are named are active.
All inputs are finite; a program needn't handle non-finite values.
Results may differ from the reference program's by a relative error of at most 0.0006.
Values may be sent and summed in bfloat16 or wider, within the bound.
No kernel may reach another device: no remote copies, remote signals or barrier semaphores. Data moves between devices by JAX's collectives and lax.ppermute only.
A program may use at most 64 MiB of HBM per device.

```python
import jax
import jax.numpy as jnp
from jax import lax

CIN = 96
CMID = 128
CLASSES = 8
BLOCK = 128
HB = 2
P_DEV = 2048
NB_DEV = 16
ROTS = 16
POINTS = 65536
VOX_DEV = 2048
VOXELS = 65536
HALO = 256
CAP = 192
N_SLAB = 32


def busy_slab(key):
    return jax.random.randint(jax.random.fold_in(key, 7), (ROTS,), 0, N_SLAB)


def active_table(key):
    lowest = max(HB, NB_DEV // 4)
    base_counts = jax.random.randint(jax.random.fold_in(key, 11), (ROTS, N_SLAB), lowest, NB_DEV + 1)
    busiest = jnp.arange(N_SLAB)[None, :] == busy_slab(key)[:, None]
    return jnp.where(busiest, NB_DEV, base_counts).astype(jnp.int32)


def owner_table(key):
    busy = busy_slab(key)
    pool_slots = jnp.arange((N_SLAB - 1) * CAP) // CAP
    flat_keys = jax.random.split(jax.random.fold_in(key, 13), ROTS * N_SLAB)
    flat_busy = jnp.repeat(busy, N_SLAB)

    def one_source(source_key, busy_one):
        first_key, second_key = jax.random.split(source_key)
        others = pool_slots + (pool_slots >= busy_one).astype(jnp.int32)
        mixed = jax.random.permutation(first_key, others)[:P_DEV - CAP]
        targets = jnp.concatenate([jnp.full((CAP,), busy_one, jnp.int32), mixed.astype(jnp.int32)])
        return jax.random.permutation(second_key, targets)
    return jax.vmap(one_source)(flat_keys, flat_busy).reshape(ROTS, POINTS).astype(jnp.int32)


def draw_owners(key, part):
    return owner_table(key)


def draw_active_count(key, part):
    return active_table(key)


def draw_voxel_ids(key, part):
    owner_rows = owner_table(key)
    active_rows = active_table(key)
    upper = jnp.take_along_axis(active_rows, owner_rows, axis=1) * BLOCK
    return jax.random.randint(jax.random.fold_in(key, 17), (ROTS, POINTS), 0, upper).astype(jnp.int32)


def draw_halo_blocks(key, part):
    active_rows = active_table(key)
    return jax.random.randint(jax.random.fold_in(key, 19), (ROTS, N_SLAB, 2, HB), 0, active_rows[:, :, None, None]).astype(jnp.int32)


def draw_neighbors(key, part):
    active_rows = active_table(key)
    voxel_slot = jnp.arange(VOXELS)
    slab_of = voxel_slot // VOX_DEV
    local_slot = voxel_slot % VOX_DEV
    upper = active_rows[:, slab_of] * BLOCK
    dims = (ROTS, 27, VOXELS)
    category = jax.random.randint(jax.random.fold_in(key, 23), dims, 0, 8)
    own_rows = jax.random.randint(jax.random.fold_in(key, 29), dims, 0, upper[:, None, :])
    lower_rows = VOX_DEV + jax.random.randint(jax.random.fold_in(key, 31), dims, 0, HALO)
    higher_rows = VOX_DEV + HALO + jax.random.randint(jax.random.fold_in(key, 37), dims, 0, HALO)
    zero_index = VOX_DEV + 2 * HALO
    picked = jnp.where(category < 2, zero_index, jnp.where(category < 6, own_rows, jnp.where(category == 6, lower_rows, higher_rows)))
    centre = jnp.arange(27)[None, :, None] == 13
    picked = jnp.where(centre, local_slot[None, None, :], picked)
    living = local_slot[None, None, :] < upper[:, None, :]
    return jnp.where(living, picked, zero_index).astype(jnp.int32)


def levels(stream_key, shape, cuts, low, high):
    gain = 1.0
    for axis_at, blocks in cuts:
        steps = jax.random.uniform(jax.random.fold_in(jax.random.fold_in(stream_key, 6), axis_at), (blocks,), jnp.float32, low / len(cuts), high / len(cuts))
        gain = gain * jnp.repeat(jnp.exp(steps), shape[axis_at] // blocks).reshape((-1,) + (1,) * (len(shape) - 1 - axis_at))
    return gain


def noise(key, shape, scale, bound, cuts=(), kind=jnp.bfloat16):
    result = jax.random.normal(key, shape, jnp.float32) * scale
    if len(cuts) > 0:
        result = levels(key, shape, cuts, -0.22, 0.18) * result
    return jnp.clip(result, min=-bound, max=bound).astype(kind)


def setup_inputs(seed: int = 0) -> dict:
    seeds = jax.random.split(jax.random.key(seed), 15)
    point_feats = noise(seeds[0], (POINTS, CIN), 1.0, 6.0, ((0, 32),))
    owners = draw_owners(jax.random.fold_in(seeds[14], 71), 0)
    voxel_ids = draw_voxel_ids(jax.random.fold_in(seeds[14], 71), 0)
    active_count = draw_active_count(jax.random.fold_in(seeds[14], 71), 0)
    halo_blocks = draw_halo_blocks(jax.random.fold_in(seeds[14], 71), 0)
    neighbors = draw_neighbors(jax.random.fold_in(seeds[14], 71), 0)
    conv1_weight = noise(seeds[6], (27, CIN, CMID), (27 * CIN) ** -0.5, 0.125)
    conv1_scale = jnp.clip(1.0 + 0.18 * jax.random.normal(seeds[7], (CMID,), jnp.float32), 0.1, 1.9)
    conv1_shift = noise(seeds[8], (CMID,), 0.5, 3.0, (), jnp.float32)
    conv2_weight = noise(seeds[9], (27, CMID, CMID), (27 * CMID) ** -0.5, 0.109375)
    conv2_scale = jnp.clip(1.0 + 0.18 * jax.random.normal(seeds[10], (CMID,), jnp.float32), 0.1, 1.9)
    conv2_shift = noise(seeds[11], (CMID,), 0.5, 3.0, (), jnp.float32)
    head_weight = noise(seeds[12], (CMID, CLASSES), CMID ** -0.5, 0.5)
    head_bias = noise(seeds[13], (CLASSES,), 1.0, 4.0, (), jnp.float32)
    return dict(point_feats=point_feats, owners=owners, voxel_ids=voxel_ids, active_count=active_count, halo_blocks=halo_blocks, neighbors=neighbors, conv1_weight=conv1_weight, conv1_scale=conv1_scale, conv1_shift=conv1_shift, conv2_weight=conv2_weight, conv2_scale=conv2_scale, conv2_shift=conv2_shift, head_weight=head_weight, head_bias=head_bias)


def extend_rows(features, halo_list):
    channels = features.shape[2]
    block_tiles = features.reshape(N_SLAB, NB_DEV, BLOCK, channels)
    upward = jax.vmap(lambda tiles_one, list_one: tiles_one[list_one[1]].reshape(HALO, channels))(block_tiles, halo_list)
    downward = jax.vmap(lambda tiles_one, list_one: tiles_one[list_one[0]].reshape(HALO, channels))(block_tiles, halo_list)
    blank = jnp.zeros((1, HALO, channels), features.dtype)
    from_below = jnp.concatenate([blank, upward[:-1]], axis=0)
    from_above = jnp.concatenate([downward[1:], blank], axis=0)
    blank_row = jnp.zeros((N_SLAB, 1, channels), features.dtype)
    return jnp.concatenate([features, from_below, from_above, blank_row], axis=1)


def convolve_slab(extended, neighbor_table, weight, scale_vec, shift_vec, residual, living):
    groups = VOX_DEV // 512
    index_groups = neighbor_table.reshape(27, groups, 512).transpose(1, 0, 2)
    weight_wide = weight.astype(jnp.float32)

    def one_group(index_rows):
        return jnp.einsum("kvc,kcd->vd", extended[index_rows].astype(jnp.float32), weight_wide)

    summed = lax.map(one_group, index_groups).reshape(VOX_DEV, -1)
    values = summed * scale_vec + shift_vec + residual.astype(jnp.float32)
    return jnp.where(living[:, None], jnp.maximum(values, 0.0), 0.0).astype(jnp.bfloat16)


def reference(point_feats, owners, voxel_ids, active_count, halo_blocks, neighbors, conv1_weight, conv1_scale, conv1_shift, conv2_weight, conv2_scale, conv2_shift, head_weight, head_bias):
    point_wide = point_feats.astype(jnp.float32)
    nothing = jnp.zeros((N_SLAB, VOX_DEV, CMID), jnp.float32)

    def one_copy(inputs):
        owner_row, voxel_row, active_row, halo_list, neighbor_table = inputs
        global_voxel = (owner_row * VOX_DEV + voxel_row).astype(jnp.int32)
        totals = jax.ops.segment_sum(point_wide, global_voxel, VOXELS)
        counts = jax.ops.segment_sum(jnp.ones((POINTS,), jnp.float32), global_voxel, VOXELS)
        voxel_in = (totals / jnp.maximum(counts, 1.0)[:, None]).astype(jnp.bfloat16).reshape(N_SLAB, VOX_DEV, CIN)
        living = jnp.arange(VOX_DEV)[None, :] < (active_row * BLOCK)[:, None]
        tables = neighbor_table.reshape(27, N_SLAB, VOX_DEV).transpose(1, 0, 2)
        hidden = lax.map(lambda pieces: convolve_slab(pieces[0], pieces[1], conv1_weight, conv1_scale, conv1_shift, pieces[2], pieces[3]), (extend_rows(voxel_in, halo_list), tables, nothing, living))
        refined = lax.map(lambda pieces: convolve_slab(pieces[0], pieces[1], conv2_weight, conv2_scale, conv2_shift, pieces[2], pieces[3]), (extend_rows(hidden, halo_list), tables, hidden, living))
        voxel_logits = jnp.dot(refined.reshape(VOXELS, CMID), head_weight, preferred_element_type=jnp.float32) + head_bias
        return voxel_logits[global_voxel].T

    copies = lax.map(one_copy, (owners, voxel_ids, active_count, halo_blocks, neighbors))
    return jnp.sum(copies, axis=0) / ROTS
```

```python
import functools

import jax
import jax.numpy as jnp
from jax import lax
from jax.experimental import pallas as pl
from jax.experimental.pallas import tpu as pltpu
from jax.sharding import PartitionSpec as P

BLOCK = 128
OFFSETS = 27
CONV_ROWS = 256
POOL_ROWS = 256
POOL_COLS = 512


def passed_along(shard, axis, by):
    devices = lax.axis_size(axis)
    pairs = [(i, i + by) for i in range(devices) if 0 <= i + by < devices]
    return lax.ppermute(shard, axis, pairs)


def extend_rows(features, halo_list):
    channels = features.shape[1]
    block_tiles = features.reshape(-1, BLOCK, channels)
    upward = block_tiles[halo_list[1]].reshape(-1, channels)
    downward = block_tiles[halo_list[0]].reshape(-1, channels)
    from_below = passed_along(upward, "slab", 1)
    from_above = passed_along(downward, "slab", -1)
    rows = features.shape[0] + from_below.shape[0] + from_above.shape[0] + 1
    padding = -rows % 8 + 1
    blank_rows = jnp.zeros((padding, channels), features.dtype)
    extended = jnp.concatenate([features, from_below, from_above, blank_rows], axis=0)
    return extended.astype(jnp.float32)


def conv_kernel(active_ref, nbr_ref, ext_ref, w_ref, scale_ref, shift_ref, *rest, has_residual):
    if has_residual:
        res_ref, out_ref, gathered_ref, acc_ref = rest
    else:
        out_ref, gathered_ref, acc_ref = rest
    rows = out_ref.shape[0]
    total = nbr_ref.shape[0] // OFFSETS
    first = pl.program_id(0) * rows
    active = active_ref[0]

    @pl.when(first < active)
    def _():
        for offset in range(OFFSETS):
            slot = offset % 2
            base = offset * total + first

            def pick(i, carry):
                row = nbr_ref[base + i]
                gathered_ref[slot, pl.ds(i, 1), :] = ext_ref[pl.ds(row, 1), :]
                return carry

            lax.fori_loop(0, rows, pick, 0, unroll=8)
            part = jnp.dot(
                gathered_ref[slot].astype(jnp.bfloat16),
                w_ref[offset],
                preferred_element_type=jnp.float32,
            )
            if offset == 0:
                acc_ref[...] = part
            else:
                acc_ref[...] += part
        values = acc_ref[...] * scale_ref[...] + shift_ref[...]
        if has_residual:
            values = values + res_ref[...].astype(jnp.float32)
        living = first + lax.broadcasted_iota(jnp.int32, values.shape, 0) < active
        out_ref[...] = jnp.where(living, jnp.maximum(values, 0.0), 0.0).astype(out_ref.dtype)

    @pl.when(first >= active)
    def _():
        out_ref[...] = jnp.zeros(out_ref.shape, out_ref.dtype)


def convolve(extended, neighbor_flat, weight, scale_vec, shift_vec, residual, active_rows):
    total = neighbor_flat.shape[0] // OFFSETS
    ext_rows, channels = extended.shape
    width = weight.shape[2]
    in_specs = [
        pl.BlockSpec((ext_rows, channels), lambda s, a, n: (0, 0)),
        pl.BlockSpec(weight.shape, lambda s, a, n: (0, 0, 0)),
        pl.BlockSpec((1, width), lambda s, a, n: (0, 0)),
        pl.BlockSpec((1, width), lambda s, a, n: (0, 0)),
    ]
    operands = [extended, weight, scale_vec.reshape(1, width), shift_vec.reshape(1, width)]
    if residual is not None:
        in_specs.append(pl.BlockSpec((CONV_ROWS, width), lambda s, a, n: (s, 0)))
        operands.append(residual)
    grid_spec = pltpu.PrefetchScalarGridSpec(
        num_scalar_prefetch=2,
        grid=(total // CONV_ROWS,),
        in_specs=in_specs,
        out_specs=pl.BlockSpec((CONV_ROWS, width), lambda s, a, n: (s, 0)),
        scratch_shapes=[
            pltpu.VMEM((2, CONV_ROWS, channels), jnp.float32),
            pltpu.VMEM((CONV_ROWS, width), jnp.float32),
        ],
    )
    return pl.pallas_call(
        functools.partial(conv_kernel, has_residual=residual is not None),
        grid_spec=grid_spec,
        out_shape=jax.ShapeDtypeStruct((total, width), jnp.bfloat16),
    )(active_rows.reshape(1), neighbor_flat, *operands)


def pool_kernel(vox_ref, feats_ref, out_ref):
    rows = out_ref.shape[0]
    first = pl.program_id(0) * rows

    @pl.when(pl.program_id(1) == 0)
    def _():
        out_ref[...] = jnp.zeros(out_ref.shape, out_ref.dtype)

    ids = first + lax.broadcasted_iota(jnp.int32, (rows, vox_ref.shape[1]), 0)
    onehot = (ids == vox_ref[...]).astype(jnp.bfloat16)
    out_ref[...] += jnp.dot(onehot, feats_ref[...], preferred_element_type=jnp.float32)


def pool(voxel_of_slot, slot_feats, voxel_total):
    slots, width = slot_feats.shape
    return pl.pallas_call(
        pool_kernel,
        grid=(voxel_total // POOL_ROWS, slots // POOL_COLS),
        in_specs=[
            pl.BlockSpec((1, POOL_COLS), lambda v, s: (0, s)),
            pl.BlockSpec((POOL_COLS, width), lambda v, s: (s, 0)),
        ],
        out_specs=pl.BlockSpec((POOL_ROWS, width), lambda v, s: (v, 0)),
        out_shape=jax.ShapeDtypeStruct((voxel_total, width), jnp.float32),
    )(voxel_of_slot.reshape(1, slots), slot_feats)


def per_device(
    point_feats,
    owners,
    voxel_ids,
    active_count,
    halo_blocks,
    neighbors,
    conv1_weight,
    conv1_scale,
    conv1_shift,
    conv2_weight,
    conv2_scale,
    conv2_shift,
    head_weight,
    head_bias,
):
    slab_count = lax.axis_size("slab")
    point_count, in_width = point_feats.shape
    capacity = 3 * point_count // slab_count
    voxel_total = neighbors.shape[2]
    owner_row = owners[0]
    voxel_row = voxel_ids[0]
    owner_hot = (owner_row[:, None] == jnp.arange(slab_count)[None, :]).astype(jnp.int32)
    earlier = jnp.cumsum(owner_hot, axis=0) - owner_hot
    ranking = jnp.sum(earlier * owner_hot, axis=1)
    slot_number = owner_row * capacity + ranking
    send_feats = (
        jnp.zeros((slab_count * capacity, in_width), jnp.bfloat16)
        .at[slot_number]
        .set(point_feats)
    )
    send_voxels = (
        jnp.full((slab_count * capacity,), voxel_total, jnp.int32).at[slot_number].set(voxel_row)
    )
    got_feats = lax.all_to_all(
        send_feats.reshape(slab_count, capacity, -1), "slab", 0, 0, tiled=True
    )
    got_voxels = lax.all_to_all(
        send_voxels.reshape(slab_count, capacity), "slab", 0, 0, tiled=True
    )
    flat_voxels = got_voxels.reshape(-1)
    slot_total = flat_voxels.shape[0]
    pool_width = -(in_width + 1) // 128 * -128
    slot_rows = jnp.concatenate(
        [
            got_feats.reshape(slot_total, in_width),
            jnp.ones((slot_total, 1), jnp.bfloat16),
            jnp.zeros((slot_total, pool_width - in_width - 1), jnp.bfloat16),
        ],
        axis=1,
    )
    pooled = pool(flat_voxels, slot_rows, voxel_total)
    totals = pooled[:, :in_width]
    counts = pooled[:, in_width]
    voxel_in = (totals / jnp.maximum(counts, 1.0)[:, None]).astype(jnp.bfloat16)
    active_rows = active_count[0, 0] * BLOCK
    halo_list = halo_blocks[0, 0]
    neighbor_flat = neighbors[0].reshape(-1)
    hidden = convolve(
        extend_rows(voxel_in, halo_list),
        neighbor_flat,
        conv1_weight,
        conv1_scale,
        conv1_shift,
        None,
        active_rows,
    )
    refined = convolve(
        extend_rows(hidden, halo_list),
        neighbor_flat,
        conv2_weight,
        conv2_scale,
        conv2_shift,
        hidden,
        active_rows,
    )
    voxel_logits = jnp.dot(refined, head_weight, preferred_element_type=jnp.float32) + head_bias
    voxel_logits = jnp.concatenate(
        [voxel_logits, jnp.zeros((1, voxel_logits.shape[1]), jnp.float32)], axis=0
    )
    slot_logits = voxel_logits[flat_voxels].reshape(slab_count, capacity, -1)
    returned = lax.all_to_all(slot_logits, "slab", 0, 0, tiled=True)
    point_logits = returned.reshape(slab_count * capacity, -1)[slot_number].T
    summed = lax.psum(point_logits, "rot")
    return summed / lax.axis_size("rot")


def solution(mesh):
    return jax.shard_map(
        per_device,
        mesh=mesh,
        in_specs=(
            P("slab", None),
            P("rot", "slab"),
            P("rot", "slab"),
            P("rot", "slab"),
            P("rot", "slab", None, None),
            P("rot", None, "slab"),
            P(),
            P(),
            P(),
            P(),
            P(),
            P(),
            P(),
            P(),
        ),
        out_specs=P(None, "slab"),
        check_vma=False,
    )
```

```python
import functools

import jax
import jax.numpy as jnp
from jax import lax
from jax.experimental import pallas as pl
from jax.experimental.pallas import tpu as pltpu
from jax.sharding import PartitionSpec as P

BLOCK = 128
OFFSETS = 27
CENTRE = 13
UNROLL = 32
CONV_ROWS = 256
POOL_ROWS = 256
POOL_COLS = 512
SLOT_WIDTH = 128
DIGIT = 64


def passed_along(shard, axis, by):
    devices = lax.axis_size(axis)
    pairs = [(i, i + by) for i in range(devices) if 0 <= i + by < devices]
    return lax.ppermute(shard, axis, pairs)


def all_summed(values, axis):
    devices = lax.axis_size(axis)
    if devices & (devices - 1):
        return lax.psum(values, axis)
    step = 1
    while step < devices:
        pairs = [(i, i ^ step) for i in range(devices)]
        values = values + lax.ppermute(values, axis, pairs)
        step *= 2
    return values


def extend_rows(features, halo_list):
    channels = features.shape[1]
    block_tiles = features.reshape(-1, BLOCK, channels)
    upward = block_tiles[halo_list[1]].reshape(-1, channels)
    downward = block_tiles[halo_list[0]].reshape(-1, channels)
    from_below = passed_along(upward, "slab", 1)
    from_above = passed_along(downward, "slab", -1)
    rows = features.shape[0] + from_below.shape[0] + from_above.shape[0] + 1
    padding = -rows % 8 + 1
    blank_rows = jnp.zeros((padding, channels), features.dtype)
    extended = jnp.concatenate([features, from_below, from_above, blank_rows], axis=0)
    return extended.astype(jnp.float32)


def conv_kernel(active_ref, nbr_ref, ext_ref, w_ref, scale_ref, shift_ref, *rest, has_residual):
    if has_residual:
        res_ref, out_ref, gathered_ref, acc_ref = rest
    else:
        out_ref, gathered_ref, acc_ref = rest
    rows = out_ref.shape[0]
    first = pl.multiple_of(pl.program_id(0) * rows, rows)
    active = active_ref[0]

    @pl.when(first < active)
    def _():
        for offset in range(OFFSETS):
            slot = offset % 2
            if offset == CENTRE:
                picked = ext_ref[pl.ds(first, rows), :]
            else:
                base = offset * rows

                def pick(i, carry):
                    row = nbr_ref[base + i]
                    gathered_ref[slot, pl.ds(i, 1), :] = ext_ref[pl.ds(row, 1), :]
                    return carry

                lax.fori_loop(0, rows, pick, 0, unroll=UNROLL)
                picked = gathered_ref[slot]
            part = jnp.dot(
                picked.astype(jnp.bfloat16),
                w_ref[offset],
                preferred_element_type=jnp.float32,
            )
            if offset == 0:
                acc_ref[...] = part
            else:
                acc_ref[...] += part
        values = acc_ref[...] * scale_ref[...] + shift_ref[...]
        if has_residual:
            values = values + res_ref[...].astype(jnp.float32)
        living = first + lax.broadcasted_iota(jnp.int32, values.shape, 0) < active
        out_ref[...] = jnp.where(living, jnp.maximum(values, 0.0), 0.0).astype(out_ref.dtype)

    @pl.when(first >= active)
    def _():
        out_ref[...] = jnp.zeros(out_ref.shape, out_ref.dtype)


def convolve(extended, neighbor_table, weight, scale_vec, shift_vec, residual, active_rows):
    total = neighbor_table.shape[1]
    steps = total // CONV_ROWS
    per_step = OFFSETS * CONV_ROWS
    step_block = -per_step // 1024 * -1024
    neighbor_steps = jnp.pad(
        neighbor_table.reshape(OFFSETS, steps, CONV_ROWS).transpose(1, 0, 2).reshape(steps, -1),
        ((0, 0), (0, step_block - per_step)),
    ).reshape(-1)
    ext_rows, channels = extended.shape
    width = weight.shape[2]
    in_specs = [
        pl.BlockSpec((step_block,), lambda s, a: (s,), memory_space=pltpu.SMEM),
        pl.BlockSpec((ext_rows, channels), lambda s, a: (0, 0)),
        pl.BlockSpec(weight.shape, lambda s, a: (0, 0, 0)),
        pl.BlockSpec((1, width), lambda s, a: (0, 0)),
        pl.BlockSpec((1, width), lambda s, a: (0, 0)),
    ]
    operands = [
        neighbor_steps,
        extended,
        weight,
        scale_vec.reshape(1, width),
        shift_vec.reshape(1, width),
    ]
    if residual is not None:
        in_specs.append(pl.BlockSpec((CONV_ROWS, width), lambda s, a: (s, 0)))
        operands.append(residual)
    grid_spec = pltpu.PrefetchScalarGridSpec(
        num_scalar_prefetch=1,
        grid=(steps,),
        in_specs=in_specs,
        out_specs=pl.BlockSpec((CONV_ROWS, width), lambda s, a: (s, 0)),
        scratch_shapes=[
            pltpu.VMEM((2, CONV_ROWS, channels), jnp.float32),
            pltpu.VMEM((CONV_ROWS, width), jnp.float32),
        ],
    )
    return pl.pallas_call(
        functools.partial(conv_kernel, has_residual=residual is not None),
        grid_spec=grid_spec,
        out_shape=jax.ShapeDtypeStruct((total, width), jnp.bfloat16),
    )(active_rows.reshape(1), *operands)


def pool_kernel(vox_ref, feats_ref, out_ref):
    rows = out_ref.shape[0]
    first = pl.program_id(0) * rows
    summed = None
    for chunk in range(vox_ref.shape[1] // POOL_COLS):
        cols = slice(chunk * POOL_COLS, (chunk + 1) * POOL_COLS)
        ids = first + lax.broadcasted_iota(jnp.int32, (rows, POOL_COLS), 0)
        onehot = (ids == vox_ref[:, cols]).astype(jnp.bfloat16)
        part = jnp.dot(onehot, feats_ref[cols, :], preferred_element_type=jnp.float32)
        summed = part if summed is None else summed + part
    out_ref[...] = summed


def pool(voxel_of_slot, slot_feats, voxel_total):
    slots, width = slot_feats.shape
    return pl.pallas_call(
        pool_kernel,
        grid=(voxel_total // POOL_ROWS,),
        in_specs=[
            pl.BlockSpec((1, slots), lambda v: (0, 0)),
            pl.BlockSpec((slots, width), lambda v: (0, 0)),
        ],
        out_specs=pl.BlockSpec((POOL_ROWS, width), lambda v: (v, 0)),
        out_shape=jax.ShapeDtypeStruct((voxel_total, width), jnp.float32),
    )(voxel_of_slot.reshape(1, slots), slot_feats)


def per_device(
    point_feats,
    owners,
    voxel_ids,
    active_count,
    halo_blocks,
    neighbors,
    conv1_weight,
    conv1_scale,
    conv1_shift,
    conv2_weight,
    conv2_scale,
    conv2_shift,
    head_weight,
    head_bias,
):
    slab_count = lax.axis_size("slab")
    point_count, in_width = point_feats.shape
    capacity = 3 * point_count // slab_count
    voxel_total = neighbors.shape[2]
    owner_row = owners[0]
    voxel_row = voxel_ids[0]
    owner_hot = (owner_row[:, None] == jnp.arange(slab_count)[None, :]).astype(jnp.int32)
    earlier = jnp.cumsum(owner_hot, axis=0) - owner_hot
    ranking = jnp.sum(earlier * owner_hot, axis=1)
    slot_number = owner_row * capacity + ranking
    digits = (voxel_row // DIGIT, voxel_row % DIGIT)
    carried = jnp.concatenate(
        [
            point_feats,
            digits[0].astype(jnp.bfloat16)[:, None],
            digits[1].astype(jnp.bfloat16)[:, None],
            jnp.ones((point_count, 1), jnp.bfloat16),
            jnp.zeros((point_count, SLOT_WIDTH - in_width - 3), jnp.bfloat16),
        ],
        axis=1,
    )
    send_rows = (
        jnp.zeros((slab_count * capacity, SLOT_WIDTH), jnp.bfloat16).at[slot_number].set(carried)
    )
    got_rows = lax.all_to_all(
        send_rows.reshape(slab_count, capacity, SLOT_WIDTH), "slab", 0, 0, tiled=True
    ).reshape(slab_count * capacity, SLOT_WIDTH)
    flat_voxels = (
        got_rows[:, in_width].astype(jnp.int32) * DIGIT
        + got_rows[:, in_width + 1].astype(jnp.int32)
    )
    pooled = pool(flat_voxels, got_rows, voxel_total)
    totals = pooled[:, :in_width]
    counts = pooled[:, in_width + 2]
    voxel_in = (totals / jnp.maximum(counts, 1.0)[:, None]).astype(jnp.bfloat16)
    active_rows = active_count[0, 0] * BLOCK
    halo_list = halo_blocks[0, 0]
    neighbor_table = neighbors[0]
    hidden = convolve(
        extend_rows(voxel_in, halo_list),
        neighbor_table,
        conv1_weight,
        conv1_scale,
        conv1_shift,
        None,
        active_rows,
    )
    refined = convolve(
        extend_rows(hidden, halo_list),
        neighbor_table,
        conv2_weight,
        conv2_scale,
        conv2_shift,
        hidden,
        active_rows,
    )
    voxel_logits = jnp.dot(refined, head_weight, preferred_element_type=jnp.float32) + head_bias
    slot_logits = voxel_logits[flat_voxels].reshape(slab_count, capacity, -1)
    returned = lax.all_to_all(slot_logits, "slab", 0, 0, tiled=True)
    point_logits = returned.reshape(slab_count * capacity, -1)[slot_number].T
    summed = all_summed(point_logits, "rot")
    return summed / lax.axis_size("rot")


def solution(mesh):
    return jax.shard_map(
        per_device,
        mesh=mesh,
        in_specs=(
            P("slab", None),
            P("rot", "slab"),
            P("rot", "slab"),
            P("rot", "slab"),
            P("rot", "slab", None, None),
            P("rot", None, "slab"),
            P(),
            P(),
            P(),
            P(),
            P(),
            P(),
            P(),
            P(),
        ),
        out_specs=P(None, "slab"),
        check_vma=False,
    )
```

```python
import functools

import jax
import jax.numpy as jnp
from jax import lax
from jax.experimental import pallas as pl
from jax.experimental.pallas import tpu as pltpu
from jax.sharding import PartitionSpec as P

BLOCK = 128
OFFSETS = 27
CENTRE = 13
UNROLL = 32
CONV_ROWS = 256
POOL_ROWS = 256
POOL_COLS = 512
DIGIT = 64


def passed_along(shard, axis, by):
    devices = lax.axis_size(axis)
    pairs = [(i, i + by) for i in range(devices) if 0 <= i + by < devices]
    return lax.ppermute(shard, axis, pairs)


def all_summed(values, axis):
    devices = lax.axis_size(axis)
    if devices & (devices - 1):
        return lax.psum(values, axis)
    step = 1
    while step < devices:
        pairs = [(i, i ^ step) for i in range(devices)]
        values = values + lax.ppermute(values, axis, pairs)
        step *= 2
    return values


def extend_rows(features, halo_list):
    channels = features.shape[1]
    block_tiles = features.reshape(-1, BLOCK, channels)
    upward = block_tiles[halo_list[1]].reshape(-1, channels)
    downward = block_tiles[halo_list[0]].reshape(-1, channels)
    from_below = passed_along(upward, "slab", 1)
    from_above = passed_along(downward, "slab", -1)
    rows = features.shape[0] + from_below.shape[0] + from_above.shape[0] + 1
    padding = -rows % 8 + 1
    blank_rows = jnp.zeros((padding, channels), features.dtype)
    extended = jnp.concatenate([features, from_below, from_above, blank_rows], axis=0)
    return extended.astype(jnp.float32)


def conv_kernel(active_ref, nbr_ref, ext_ref, w_ref, scale_ref, shift_ref, *rest, has_residual):
    if has_residual:
        res_ref, out_ref, gathered_ref, acc_ref = rest
    else:
        out_ref, gathered_ref, acc_ref = rest
    rows = out_ref.shape[0]
    first = pl.multiple_of(pl.program_id(0) * rows, rows)
    active = active_ref[0]

    @pl.when(first < active)
    def _():
        for offset in range(OFFSETS):
            slot = offset % 2
            if offset == CENTRE:
                picked = ext_ref[pl.ds(first, rows), :]
            else:
                base = offset * rows

                def pick(i, carry):
                    row = nbr_ref[base + i]
                    gathered_ref[slot, pl.ds(i, 1), :] = ext_ref[pl.ds(row, 1), :]
                    return carry

                lax.fori_loop(0, rows, pick, 0, unroll=True)
                picked = gathered_ref[slot]
            part = jnp.dot(
                picked.astype(jnp.bfloat16),
                w_ref[offset],
                preferred_element_type=jnp.float32,
            )
            if offset == 0:
                acc_ref[...] = part
            else:
                acc_ref[...] += part
        values = acc_ref[...] * scale_ref[...] + shift_ref[...]
        if has_residual:
            values = values + res_ref[...].astype(jnp.float32)
        living = first + lax.broadcasted_iota(jnp.int32, values.shape, 0) < active
        out_ref[...] = jnp.where(living, jnp.maximum(values, 0.0), 0.0).astype(out_ref.dtype)

    @pl.when(first >= active)
    def _():
        out_ref[...] = jnp.zeros(out_ref.shape, out_ref.dtype)


def convolve(extended, neighbor_table, weight, scale_vec, shift_vec, residual, active_rows):
    total = neighbor_table.shape[1]
    steps = total // CONV_ROWS
    per_step = OFFSETS * CONV_ROWS
    step_block = -per_step // 1024 * -1024
    neighbor_steps = jnp.pad(
        neighbor_table.reshape(OFFSETS, steps, CONV_ROWS).transpose(1, 0, 2).reshape(steps, -1),
        ((0, 0), (0, step_block - per_step)),
    ).reshape(-1)
    ext_rows, channels = extended.shape
    width = weight.shape[2]
    in_specs = [
        pl.BlockSpec((step_block,), lambda s, a: (s,), memory_space=pltpu.SMEM),
        pl.BlockSpec((ext_rows, channels), lambda s, a: (0, 0)),
        pl.BlockSpec(weight.shape, lambda s, a: (0, 0, 0)),
        pl.BlockSpec((1, width), lambda s, a: (0, 0)),
        pl.BlockSpec((1, width), lambda s, a: (0, 0)),
    ]
    operands = [
        neighbor_steps,
        extended,
        weight,
        scale_vec.reshape(1, width),
        shift_vec.reshape(1, width),
    ]
    if residual is not None:
        in_specs.append(pl.BlockSpec((CONV_ROWS, width), lambda s, a: (s, 0)))
        operands.append(residual)
    grid_spec = pltpu.PrefetchScalarGridSpec(
        num_scalar_prefetch=1,
        grid=(steps,),
        in_specs=in_specs,
        out_specs=pl.BlockSpec((CONV_ROWS, width), lambda s, a: (s, 0)),
        scratch_shapes=[
            pltpu.VMEM((2, CONV_ROWS, channels), jnp.float32),
            pltpu.VMEM((CONV_ROWS, width), jnp.float32),
        ],
    )
    return pl.pallas_call(
        functools.partial(conv_kernel, has_residual=residual is not None),
        grid_spec=grid_spec,
        out_shape=jax.ShapeDtypeStruct((total, width), jnp.bfloat16),
    )(active_rows.reshape(1), *operands)


def pool_kernel(vox_ref, feats_ref, out_ref):
    rows = out_ref.shape[0]
    first = pl.program_id(0) * rows
    summed = None
    for chunk in range(vox_ref.shape[1] // POOL_COLS):
        cols = slice(chunk * POOL_COLS, (chunk + 1) * POOL_COLS)
        ids = first + lax.broadcasted_iota(jnp.int32, (rows, POOL_COLS), 0)
        onehot = (ids == vox_ref[:, cols]).astype(jnp.bfloat16)
        part = jnp.dot(onehot, feats_ref[cols, :], preferred_element_type=jnp.float32)
        summed = part if summed is None else summed + part
    out_ref[...] = summed


def pool(voxel_of_slot, slot_feats, voxel_total):
    slots, width = slot_feats.shape
    return pl.pallas_call(
        pool_kernel,
        grid=(voxel_total // POOL_ROWS,),
        in_specs=[
            pl.BlockSpec((1, slots), lambda v: (0, 0)),
            pl.BlockSpec((slots, width), lambda v: (0, 0)),
        ],
        out_specs=pl.BlockSpec((POOL_ROWS, width), lambda v: (v, 0)),
        out_shape=jax.ShapeDtypeStruct((voxel_total, width), jnp.float32),
    )(voxel_of_slot.reshape(1, slots), slot_feats)


def per_device(
    point_feats,
    owners,
    voxel_ids,
    active_count,
    halo_blocks,
    neighbors,
    conv1_weight,
    conv1_scale,
    conv1_shift,
    conv2_weight,
    conv2_scale,
    conv2_shift,
    head_weight,
    head_bias,
):
    slab_count = lax.axis_size("slab")
    point_count, in_width = point_feats.shape
    capacity = 3 * point_count // slab_count
    voxel_total = neighbors.shape[2]
    owner_row = owners[0]
    voxel_row = voxel_ids[0]
    owner_hot = (owner_row[:, None] == jnp.arange(slab_count)[None, :]).astype(jnp.int32)
    earlier = jnp.cumsum(owner_hot, axis=0) - owner_hot
    ranking = jnp.sum(earlier * owner_hot, axis=1)
    slot_number = owner_row * capacity + ranking
    digits = (voxel_row // DIGIT, voxel_row % DIGIT)
    carried = jnp.concatenate(
        [
            point_feats,
            digits[0].astype(jnp.bfloat16)[:, None],
            digits[1].astype(jnp.bfloat16)[:, None],
            jnp.ones((point_count, 1), jnp.bfloat16),
        ],
        axis=1,
    )
    row_width = carried.shape[1]
    send_rows = (
        jnp.zeros((slab_count * capacity, row_width), jnp.bfloat16).at[slot_number].set(carried)
    )
    chunk = capacity * row_width
    dense = -chunk // 128 * -128
    packed = jnp.pad(send_rows.reshape(slab_count, chunk), ((0, 0), (0, dense - chunk)))
    got_packed = lax.all_to_all(
        packed.reshape(slab_count, dense // 128, 128), "slab", 0, 0, tiled=True
    )
    got_rows = got_packed.reshape(slab_count, dense)[:, :chunk].reshape(-1, row_width)
    flat_voxels = (
        got_rows[:, in_width].astype(jnp.int32) * DIGIT
        + got_rows[:, in_width + 1].astype(jnp.int32)
    )
    pooled = pool(flat_voxels, got_rows, voxel_total)
    totals = pooled[:, :in_width]
    counts = pooled[:, in_width + 2]
    voxel_in = (totals / jnp.maximum(counts, 1.0)[:, None]).astype(jnp.bfloat16)
    active_rows = active_count[0, 0] * BLOCK
    halo_list = halo_blocks[0, 0]
    neighbor_table = neighbors[0]
    hidden = convolve(
        extend_rows(voxel_in, halo_list),
        neighbor_table,
        conv1_weight,
        conv1_scale,
        conv1_shift,
        None,
        active_rows,
    )
    refined = convolve(
        extend_rows(hidden, halo_list),
        neighbor_table,
        conv2_weight,
        conv2_scale,
        conv2_shift,
        hidden,
        active_rows,
    )
    voxel_logits = jnp.dot(refined, head_weight, preferred_element_type=jnp.float32) + head_bias
    slot_logits = voxel_logits[flat_voxels].reshape(slab_count, capacity, -1)
    returned = lax.all_to_all(slot_logits, "slab", 0, 0, tiled=True)
    point_logits = returned.reshape(slab_count * capacity, -1)[slot_number].T
    summed = all_summed(point_logits, "rot")
    return summed / lax.axis_size("rot")


def solution(mesh):
    return jax.shard_map(
        per_device,
        mesh=mesh,
        in_specs=(
            P("slab", None),
            P("rot", "slab"),
            P("rot", "slab"),
            P("rot", "slab"),
            P("rot", "slab", None, None),
            P("rot", None, "slab"),
            P(),
            P(),
            P(),
            P(),
            P(),
            P(),
            P(),
            P(),
        ),
        out_specs=P(None, "slab"),
        check_vma=False,
    )
```

```python
import functools

import jax
import jax.numpy as jnp
from jax import lax
from jax.experimental import pallas as pl
from jax.experimental.pallas import tpu as pltpu
from jax.sharding import PartitionSpec as P

BLOCK = 128
OFFSETS = 27
CENTRE = 13
UNROLL = 32
CONV_ROWS = 256
POOL_ROWS = 256
POOL_COLS = 512
DIGIT = 64


def passed_along(shard, axis, by):
    devices = lax.axis_size(axis)
    pairs = [(i, i + by) for i in range(devices) if 0 <= i + by < devices]
    return lax.ppermute(shard, axis, pairs)


def all_summed(values, axis):
    devices = lax.axis_size(axis)
    if devices & (devices - 1):
        return lax.psum(values, axis)

    def partner(by):
        return lax.ppermute(values, axis, [(i, i ^ by) for i in range(devices)])

    step = 1
    while step < devices:
        if step * 4 <= devices:
            values = (values + partner(step)) + (partner(2 * step) + partner(3 * step))
            step *= 4
        else:
            values = values + partner(step)
            step *= 2
    return values


def extend_rows(features, halo_list):
    channels = features.shape[1]
    block_tiles = features.reshape(-1, BLOCK, channels)
    upward = block_tiles[halo_list[1]].reshape(-1, channels)
    downward = block_tiles[halo_list[0]].reshape(-1, channels)
    from_below = passed_along(upward, "slab", 1)
    from_above = passed_along(downward, "slab", -1)
    rows = features.shape[0] + from_below.shape[0] + from_above.shape[0] + 1
    padding = -rows % 8 + 1
    blank_rows = jnp.zeros((padding, channels), features.dtype)
    extended = jnp.concatenate([features, from_below, from_above, blank_rows], axis=0)
    return extended.astype(jnp.float32)


def conv_kernel(active_ref, nbr_ref, ext_ref, w_ref, scale_ref, shift_ref, *rest, has_residual):
    if has_residual:
        res_ref, out_ref, gathered_ref, acc_ref = rest
    else:
        out_ref, gathered_ref, acc_ref = rest
    rows = out_ref.shape[0]
    first = pl.multiple_of(pl.program_id(0) * rows, rows)
    active = active_ref[0]

    @pl.when(first < active)
    def _():
        for offset in range(OFFSETS):
            slot = offset % 2
            if offset == CENTRE:
                picked = ext_ref[pl.ds(first, rows), :]
            else:
                base = offset * rows

                def pick(i, carry):
                    row = nbr_ref[base + i]
                    gathered_ref[slot, pl.ds(i, 1), :] = ext_ref[pl.ds(row, 1), :]
                    return carry

                lax.fori_loop(0, rows, pick, 0, unroll=True)
                picked = gathered_ref[slot]
            part = jnp.dot(
                picked.astype(jnp.bfloat16),
                w_ref[offset],
                preferred_element_type=jnp.float32,
            )
            if offset == 0:
                acc_ref[...] = part
            else:
                acc_ref[...] += part
        values = acc_ref[...] * scale_ref[...] + shift_ref[...]
        if has_residual:
            values = values + res_ref[...].astype(jnp.float32)
        living = first + lax.broadcasted_iota(jnp.int32, values.shape, 0) < active
        out_ref[...] = jnp.where(living, jnp.maximum(values, 0.0), 0.0).astype(out_ref.dtype)

    @pl.when(first >= active)
    def _():
        out_ref[...] = jnp.zeros(out_ref.shape, out_ref.dtype)


def convolve(extended, neighbor_table, weight, scale_vec, shift_vec, residual, active_rows):
    total = neighbor_table.shape[1]
    steps = total // CONV_ROWS
    per_step = OFFSETS * CONV_ROWS
    step_block = -per_step // 1024 * -1024
    neighbor_steps = jnp.pad(
        neighbor_table.reshape(OFFSETS, steps, CONV_ROWS).transpose(1, 0, 2).reshape(steps, -1),
        ((0, 0), (0, step_block - per_step)),
    ).reshape(-1)
    ext_rows, channels = extended.shape
    width = weight.shape[2]
    in_specs = [
        pl.BlockSpec((step_block,), lambda s, a: (s,), memory_space=pltpu.SMEM),
        pl.BlockSpec((ext_rows, channels), lambda s, a: (0, 0)),
        pl.BlockSpec(weight.shape, lambda s, a: (0, 0, 0)),
        pl.BlockSpec((1, width), lambda s, a: (0, 0)),
        pl.BlockSpec((1, width), lambda s, a: (0, 0)),
    ]
    operands = [
        neighbor_steps,
        extended,
        weight,
        scale_vec.reshape(1, width),
        shift_vec.reshape(1, width),
    ]
    if residual is not None:
        in_specs.append(pl.BlockSpec((CONV_ROWS, width), lambda s, a: (s, 0)))
        operands.append(residual)
    grid_spec = pltpu.PrefetchScalarGridSpec(
        num_scalar_prefetch=1,
        grid=(steps,),
        in_specs=in_specs,
        out_specs=pl.BlockSpec((CONV_ROWS, width), lambda s, a: (s, 0)),
        scratch_shapes=[
            pltpu.VMEM((2, CONV_ROWS, channels), jnp.float32),
            pltpu.VMEM((CONV_ROWS, width), jnp.float32),
        ],
    )
    return pl.pallas_call(
        functools.partial(conv_kernel, has_residual=residual is not None),
        grid_spec=grid_spec,
        out_shape=jax.ShapeDtypeStruct((total, width), jnp.bfloat16),
    )(active_rows.reshape(1), *operands)


def pool_kernel(vox_ref, feats_ref, out_ref):
    rows = out_ref.shape[0]
    first = pl.program_id(0) * rows
    summed = None
    for chunk in range(vox_ref.shape[1] // POOL_COLS):
        cols = slice(chunk * POOL_COLS, (chunk + 1) * POOL_COLS)
        ids = first + lax.broadcasted_iota(jnp.int32, (rows, POOL_COLS), 0)
        onehot = (ids == vox_ref[:, cols]).astype(jnp.bfloat16)
        part = jnp.dot(onehot, feats_ref[cols, :], preferred_element_type=jnp.float32)
        summed = part if summed is None else summed + part
    out_ref[...] = summed


def pool(voxel_of_slot, slot_feats, voxel_total):
    slots, width = slot_feats.shape
    return pl.pallas_call(
        pool_kernel,
        grid=(voxel_total // POOL_ROWS,),
        in_specs=[
            pl.BlockSpec((1, slots), lambda v: (0, 0)),
            pl.BlockSpec((slots, width), lambda v: (0, 0)),
        ],
        out_specs=pl.BlockSpec((POOL_ROWS, width), lambda v: (v, 0)),
        out_shape=jax.ShapeDtypeStruct((voxel_total, width), jnp.float32),
    )(voxel_of_slot.reshape(1, slots), slot_feats)


def gather_kernel(index_ref, table_ref, out_ref):
    def pick(i, carry):
        out_ref[pl.ds(i, 1), :] = table_ref[pl.ds(index_ref[i], 1), :]
        return carry

    lax.fori_loop(0, out_ref.shape[0], pick, 0, unroll=64)


def gather_rows(table, index):
    return pl.pallas_call(
        gather_kernel,
        in_specs=[
            pl.BlockSpec(memory_space=pltpu.SMEM),
            pl.BlockSpec(memory_space=pltpu.VMEM),
        ],
        out_specs=pl.BlockSpec(memory_space=pltpu.VMEM),
        out_shape=jax.ShapeDtypeStruct((index.shape[0], table.shape[1]), table.dtype),
    )(index, table)


def per_device(
    point_feats,
    owners,
    voxel_ids,
    active_count,
    halo_blocks,
    neighbors,
    conv1_weight,
    conv1_scale,
    conv1_shift,
    conv2_weight,
    conv2_scale,
    conv2_shift,
    head_weight,
    head_bias,
):
    slab_count = lax.axis_size("slab")
    point_count, in_width = point_feats.shape
    capacity = 3 * point_count // slab_count
    voxel_total = neighbors.shape[2]
    owner_row = owners[0]
    voxel_row = voxel_ids[0]
    owner_hot = (owner_row[:, None] == jnp.arange(slab_count)[None, :]).astype(jnp.int32)
    earlier = jnp.cumsum(owner_hot, axis=0) - owner_hot
    ranking = jnp.sum(earlier * owner_hot, axis=1)
    slot_number = owner_row * capacity + ranking
    digits = (voxel_row // DIGIT, voxel_row % DIGIT)
    carried = jnp.concatenate(
        [
            point_feats,
            digits[0].astype(jnp.bfloat16)[:, None],
            digits[1].astype(jnp.bfloat16)[:, None],
            jnp.ones((point_count, 1), jnp.bfloat16),
        ],
        axis=1,
    )
    row_width = carried.shape[1]
    send_rows = (
        jnp.zeros((slab_count * capacity, row_width), jnp.bfloat16).at[slot_number].set(carried)
    )
    chunk = capacity * row_width
    dense = -chunk // 128 * -128
    packed = jnp.pad(send_rows.reshape(slab_count, chunk), ((0, 0), (0, dense - chunk)))
    got_packed = lax.all_to_all(
        packed.reshape(slab_count, dense // 128, 128), "slab", 0, 0, tiled=True
    )
    got_rows = got_packed.reshape(slab_count, dense)[:, :chunk].reshape(-1, row_width)
    flat_voxels = (
        got_rows[:, in_width].astype(jnp.int32) * DIGIT
        + got_rows[:, in_width + 1].astype(jnp.int32)
    )
    pooled = pool(flat_voxels, got_rows, voxel_total)
    totals = pooled[:, :in_width]
    counts = pooled[:, in_width + 2]
    voxel_in = (totals / jnp.maximum(counts, 1.0)[:, None]).astype(jnp.bfloat16)
    active_rows = active_count[0, 0] * BLOCK
    halo_list = halo_blocks[0, 0]
    neighbor_table = neighbors[0]
    hidden = convolve(
        extend_rows(voxel_in, halo_list),
        neighbor_table,
        conv1_weight,
        conv1_scale,
        conv1_shift,
        None,
        active_rows,
    )
    refined = convolve(
        extend_rows(hidden, halo_list),
        neighbor_table,
        conv2_weight,
        conv2_scale,
        conv2_shift,
        hidden,
        active_rows,
    )
    voxel_logits = jnp.dot(refined, head_weight, preferred_element_type=jnp.float32) + head_bias
    slot_logits = gather_rows(voxel_logits, flat_voxels).reshape(slab_count, capacity, -1)
    returned = lax.all_to_all(slot_logits, "slab", 0, 0, tiled=True)
    point_logits = gather_rows(returned.reshape(slab_count * capacity, -1), slot_number).T
    summed = all_summed(point_logits, "rot")
    return summed / lax.axis_size("rot")


def solution(mesh):
    return jax.shard_map(
        per_device,
        mesh=mesh,
        in_specs=(
            P("slab", None),
            P("rot", "slab"),
            P("rot", "slab"),
            P("rot", "slab"),
            P("rot", "slab", None, None),
            P("rot", None, "slab"),
            P(),
            P(),
            P(),
            P(),
            P(),
            P(),
            P(),
            P(),
        ),
        out_specs=P(None, "slab"),
        check_vma=False,
    )
```

```python
import functools

import jax
import jax.numpy as jnp
from jax import lax
from jax.experimental import pallas as pl
from jax.experimental.pallas import tpu as pltpu
from jax.sharding import PartitionSpec as P

BLOCK = 128
OFFSETS = 27
CENTRE = 13
UNROLL = 32
CONV_ROWS = 256
POOL_ROWS = 256
POOL_COLS = 512
DIGIT = 64


def passed_along(shard, axis, by):
    devices = lax.axis_size(axis)
    pairs = [(i, i + by) for i in range(devices) if 0 <= i + by < devices]
    return lax.ppermute(shard, axis, pairs)


def all_summed(values, axis):
    devices = lax.axis_size(axis)
    if devices & (devices - 1):
        return lax.psum(values, axis)
    step = 1
    while step < devices:
        pairs = [(i, i ^ step) for i in range(devices)]
        values = values + lax.ppermute(values, axis, pairs)
        step *= 2
    return values


def extend_rows(features, halo_list):
    channels = features.shape[1]
    block_tiles = features.reshape(-1, BLOCK, channels)
    upward = block_tiles[halo_list[1]].reshape(-1, channels)
    downward = block_tiles[halo_list[0]].reshape(-1, channels)
    from_below = passed_along(upward, "slab", 1)
    from_above = passed_along(downward, "slab", -1)
    rows = features.shape[0] + from_below.shape[0] + from_above.shape[0] + 1
    padding = -rows % 8 + 1
    blank_rows = jnp.zeros((padding, channels), features.dtype)
    extended = jnp.concatenate([features, from_below, from_above, blank_rows], axis=0)
    return extended.astype(jnp.float32)


def conv_kernel(active_ref, nbr_ref, ext_ref, w_ref, scale_ref, shift_ref, *rest, has_residual):
    if has_residual:
        res_ref, out_ref, gathered_ref = rest
    else:
        out_ref, gathered_ref = rest
    rows = out_ref.shape[0]
    channels = ext_ref.shape[1]
    first = pl.multiple_of(pl.program_id(0) * rows, rows)
    active = active_ref[0]

    @pl.when(first < active)
    def _():
        for offset in range(OFFSETS):
            lanes = pl.ds(offset * channels, channels)
            if offset == CENTRE:
                gathered_ref[:, lanes] = ext_ref[pl.ds(first, rows), :]
                continue
            base = offset * rows

            def pick(i, carry):
                row = nbr_ref[base + i]
                gathered_ref[pl.ds(i, 1), lanes] = ext_ref[pl.ds(row, 1), :]
                return carry

            lax.fori_loop(0, rows, pick, 0, unroll=True)
        summed = jnp.dot(
            gathered_ref[...].astype(jnp.bfloat16), w_ref[...], preferred_element_type=jnp.float32
        )
        values = summed * scale_ref[...] + shift_ref[...]
        if has_residual:
            values = values + res_ref[...].astype(jnp.float32)
        living = first + lax.broadcasted_iota(jnp.int32, values.shape, 0) < active
        out_ref[...] = jnp.where(living, jnp.maximum(values, 0.0), 0.0).astype(out_ref.dtype)

    @pl.when(first >= active)
    def _():
        out_ref[...] = jnp.zeros(out_ref.shape, out_ref.dtype)


def convolve(extended, neighbor_table, weight, scale_vec, shift_vec, residual, active_rows):
    total = neighbor_table.shape[1]
    steps = total // CONV_ROWS
    per_step = OFFSETS * CONV_ROWS
    step_block = -per_step // 1024 * -1024
    neighbor_steps = jnp.pad(
        neighbor_table.reshape(OFFSETS, steps, CONV_ROWS).transpose(1, 0, 2).reshape(steps, -1),
        ((0, 0), (0, step_block - per_step)),
    ).reshape(-1)
    ext_rows, width_in = extended.shape
    channels = -width_in // 128 * -128
    width = weight.shape[2]
    extended = jnp.pad(extended, ((0, 0), (0, channels - width_in)))
    weight_flat = jnp.pad(weight, ((0, 0), (0, channels - width_in), (0, 0))).reshape(-1, width)
    in_specs = [
        pl.BlockSpec((step_block,), lambda s, a: (s,), memory_space=pltpu.SMEM),
        pl.BlockSpec((ext_rows, channels), lambda s, a: (0, 0)),
        pl.BlockSpec(weight_flat.shape, lambda s, a: (0, 0)),
        pl.BlockSpec((1, width), lambda s, a: (0, 0)),
        pl.BlockSpec((1, width), lambda s, a: (0, 0)),
    ]
    operands = [
        neighbor_steps,
        extended,
        weight_flat,
        scale_vec.reshape(1, width),
        shift_vec.reshape(1, width),
    ]
    if residual is not None:
        in_specs.append(pl.BlockSpec((CONV_ROWS, width), lambda s, a: (s, 0)))
        operands.append(residual)
    grid_spec = pltpu.PrefetchScalarGridSpec(
        num_scalar_prefetch=1,
        grid=(steps,),
        in_specs=in_specs,
        out_specs=pl.BlockSpec((CONV_ROWS, width), lambda s, a: (s, 0)),
        scratch_shapes=[pltpu.VMEM((CONV_ROWS, OFFSETS * channels), jnp.float32)],
    )
    return pl.pallas_call(
        functools.partial(conv_kernel, has_residual=residual is not None),
        grid_spec=grid_spec,
        out_shape=jax.ShapeDtypeStruct((total, width), jnp.bfloat16),
    )(active_rows.reshape(1), *operands)


def pool_kernel(vox_ref, feats_ref, out_ref):
    rows = out_ref.shape[0]
    first = pl.program_id(0) * rows
    summed = None
    for chunk in range(vox_ref.shape[1] // POOL_COLS):
        cols = slice(chunk * POOL_COLS, (chunk + 1) * POOL_COLS)
        ids = first + lax.broadcasted_iota(jnp.int32, (rows, POOL_COLS), 0)
        onehot = (ids == vox_ref[:, cols]).astype(jnp.bfloat16)
        part = jnp.dot(onehot, feats_ref[cols, :], preferred_element_type=jnp.float32)
        summed = part if summed is None else summed + part
    out_ref[...] = summed


def pool(voxel_of_slot, slot_feats, voxel_total):
    slots, width = slot_feats.shape
    return pl.pallas_call(
        pool_kernel,
        grid=(voxel_total // POOL_ROWS,),
        in_specs=[
            pl.BlockSpec((1, slots), lambda v: (0, 0)),
            pl.BlockSpec((slots, width), lambda v: (0, 0)),
        ],
        out_specs=pl.BlockSpec((POOL_ROWS, width), lambda v: (v, 0)),
        out_shape=jax.ShapeDtypeStruct((voxel_total, width), jnp.float32),
    )(voxel_of_slot.reshape(1, slots), slot_feats)


def gather_kernel(index_ref, table_ref, out_ref):
    def pick(i, carry):
        out_ref[pl.ds(i, 1), :] = table_ref[pl.ds(index_ref[i], 1), :]
        return carry

    lax.fori_loop(0, out_ref.shape[0], pick, 0, unroll=64)


def gather_rows(table, index):
    return pl.pallas_call(
        gather_kernel,
        in_specs=[
            pl.BlockSpec(memory_space=pltpu.SMEM),
            pl.BlockSpec(memory_space=pltpu.VMEM),
        ],
        out_specs=pl.BlockSpec(memory_space=pltpu.VMEM),
        out_shape=jax.ShapeDtypeStruct((index.shape[0], table.shape[1]), table.dtype),
    )(index, table)


def per_device(
    point_feats,
    owners,
    voxel_ids,
    active_count,
    halo_blocks,
    neighbors,
    conv1_weight,
    conv1_scale,
    conv1_shift,
    conv2_weight,
    conv2_scale,
    conv2_shift,
    head_weight,
    head_bias,
):
    slab_count = lax.axis_size("slab")
    point_count, in_width = point_feats.shape
    capacity = 3 * point_count // slab_count
    voxel_total = neighbors.shape[2]
    owner_row = owners[0]
    voxel_row = voxel_ids[0]
    owner_hot = (owner_row[:, None] == jnp.arange(slab_count)[None, :]).astype(jnp.int32)
    earlier = jnp.cumsum(owner_hot, axis=0) - owner_hot
    ranking = jnp.sum(earlier * owner_hot, axis=1)
    slot_number = owner_row * capacity + ranking
    digits = (voxel_row // DIGIT, voxel_row % DIGIT)
    carried = jnp.concatenate(
        [
            point_feats,
            digits[0].astype(jnp.bfloat16)[:, None],
            digits[1].astype(jnp.bfloat16)[:, None],
            jnp.ones((point_count, 1), jnp.bfloat16),
        ],
        axis=1,
    )
    row_width = carried.shape[1]
    send_rows = (
        jnp.zeros((slab_count * capacity, row_width), jnp.bfloat16).at[slot_number].set(carried)
    )
    chunk = capacity * row_width
    dense = -chunk // 128 * -128
    packed = jnp.pad(send_rows.reshape(slab_count, chunk), ((0, 0), (0, dense - chunk)))
    got_packed = lax.all_to_all(
        packed.reshape(slab_count, dense // 128, 128), "slab", 0, 0, tiled=True
    )
    got_rows = got_packed.reshape(slab_count, dense)[:, :chunk].reshape(-1, row_width)
    flat_voxels = (
        got_rows[:, in_width].astype(jnp.int32) * DIGIT
        + got_rows[:, in_width + 1].astype(jnp.int32)
    )
    pooled = pool(flat_voxels, got_rows, voxel_total)
    totals = pooled[:, :in_width]
    counts = pooled[:, in_width + 2]
    voxel_in = (totals / jnp.maximum(counts, 1.0)[:, None]).astype(jnp.bfloat16)
    active_rows = active_count[0, 0] * BLOCK
    halo_list = halo_blocks[0, 0]
    neighbor_table = neighbors[0]
    hidden = convolve(
        extend_rows(voxel_in, halo_list),
        neighbor_table,
        conv1_weight,
        conv1_scale,
        conv1_shift,
        None,
        active_rows,
    )
    refined = convolve(
        extend_rows(hidden, halo_list),
        neighbor_table,
        conv2_weight,
        conv2_scale,
        conv2_shift,
        hidden,
        active_rows,
    )
    voxel_logits = jnp.dot(refined, head_weight, preferred_element_type=jnp.float32) + head_bias
    slot_logits = gather_rows(voxel_logits, flat_voxels).reshape(slab_count, capacity, -1)
    returned = lax.all_to_all(slot_logits, "slab", 0, 0, tiled=True)
    point_logits = gather_rows(returned.reshape(slab_count * capacity, -1), slot_number).T
    summed = all_summed(point_logits, "rot")
    return summed / lax.axis_size("rot")


def solution(mesh):
    return jax.shard_map(
        per_device,
        mesh=mesh,
        in_specs=(
            P("slab", None),
            P("rot", "slab"),
            P("rot", "slab"),
            P("rot", "slab"),
            P("rot", "slab", None, None),
            P("rot", None, "slab"),
            P(),
            P(),
            P(),
            P(),
            P(),
            P(),
            P(),
            P(),
        ),
        out_specs=P(None, "slab"),
        check_vma=False,
    )
```

```python
import functools

import jax
import jax.numpy as jnp
from jax import lax
from jax.experimental import pallas as pl
from jax.experimental.pallas import tpu as pltpu
from jax.sharding import PartitionSpec as P

BLOCK = 128
OFFSETS = 27
CENTRE = 13
UNROLL = 32
CONV_ROWS = 256
POOL_ROWS = 256
POOL_COLS = 512
DIGIT = 64
RANK_BLOCK = 128


def passed_along(shard, axis, by):
    devices = lax.axis_size(axis)
    pairs = [(i, i + by) for i in range(devices) if 0 <= i + by < devices]
    return lax.ppermute(shard, axis, pairs)


def all_summed(values, axis):
    devices = lax.axis_size(axis)
    if devices & (devices - 1):
        return lax.psum(values, axis)
    step = 1
    while step < devices:
        pairs = [(i, i ^ step) for i in range(devices)]
        values = values + lax.ppermute(values, axis, pairs)
        step *= 2
    return values


def extend_rows(features, halo_list):
    channels = features.shape[1]
    block_tiles = features.reshape(-1, BLOCK, channels)
    upward = block_tiles[halo_list[1]].reshape(-1, channels)
    downward = block_tiles[halo_list[0]].reshape(-1, channels)
    from_below = passed_along(upward, "slab", 1)
    from_above = passed_along(downward, "slab", -1)
    rows = features.shape[0] + from_below.shape[0] + from_above.shape[0] + 1
    padding = -rows % 8 + 1
    blank_rows = jnp.zeros((padding, channels), features.dtype)
    extended = jnp.concatenate([features, from_below, from_above, blank_rows], axis=0)
    return extended.astype(jnp.float32)


def conv_kernel(active_ref, nbr_ref, ext_ref, w_ref, scale_ref, shift_ref, *rest, has_residual):
    if has_residual:
        res_ref, out_ref, gathered_ref = rest
    else:
        out_ref, gathered_ref = rest
    rows = out_ref.shape[0]
    channels = ext_ref.shape[1]
    first = pl.multiple_of(pl.program_id(0) * rows, rows)
    active = active_ref[0]

    @pl.when(first < active)
    def _():
        for offset in range(OFFSETS):
            lanes = pl.ds(offset * channels, channels)
            if offset == CENTRE:
                gathered_ref[:, lanes] = ext_ref[pl.ds(first, rows), :]
                continue
            base = offset * rows

            def pick(i, carry):
                row = nbr_ref[base + i]
                gathered_ref[pl.ds(i, 1), lanes] = ext_ref[pl.ds(row, 1), :]
                return carry

            lax.fori_loop(0, rows, pick, 0, unroll=True)
        summed = jnp.dot(
            gathered_ref[...].astype(jnp.bfloat16), w_ref[...], preferred_element_type=jnp.float32
        )
        values = summed * scale_ref[...] + shift_ref[...]
        if has_residual:
            values = values + res_ref[...].astype(jnp.float32)
        living = first + lax.broadcasted_iota(jnp.int32, values.shape, 0) < active
        out_ref[...] = jnp.where(living, jnp.maximum(values, 0.0), 0.0).astype(out_ref.dtype)

    @pl.when(first >= active)
    def _():
        out_ref[...] = jnp.zeros(out_ref.shape, out_ref.dtype)


def convolve(extended, neighbor_table, weight, scale_vec, shift_vec, residual, active_rows):
    total = neighbor_table.shape[1]
    steps = total // CONV_ROWS
    per_step = OFFSETS * CONV_ROWS
    step_block = -per_step // 1024 * -1024
    neighbor_steps = jnp.pad(
        neighbor_table.reshape(OFFSETS, steps, CONV_ROWS).transpose(1, 0, 2).reshape(steps, -1),
        ((0, 0), (0, step_block - per_step)),
    ).reshape(-1)
    ext_rows, width_in = extended.shape
    channels = -width_in // 128 * -128
    width = weight.shape[2]
    extended = jnp.pad(extended, ((0, 0), (0, channels - width_in)))
    weight_flat = jnp.pad(weight, ((0, 0), (0, channels - width_in), (0, 0))).reshape(-1, width)
    in_specs = [
        pl.BlockSpec((step_block,), lambda s, a: (s,), memory_space=pltpu.SMEM),
        pl.BlockSpec((ext_rows, channels), lambda s, a: (0, 0)),
        pl.BlockSpec(weight_flat.shape, lambda s, a: (0, 0)),
        pl.BlockSpec((1, width), lambda s, a: (0, 0)),
        pl.BlockSpec((1, width), lambda s, a: (0, 0)),
    ]
    operands = [
        neighbor_steps,
        extended,
        weight_flat,
        scale_vec.reshape(1, width),
        shift_vec.reshape(1, width),
    ]
    if residual is not None:
        in_specs.append(pl.BlockSpec((CONV_ROWS, width), lambda s, a: (s, 0)))
        operands.append(residual)
    grid_spec = pltpu.PrefetchScalarGridSpec(
        num_scalar_prefetch=1,
        grid=(steps,),
        in_specs=in_specs,
        out_specs=pl.BlockSpec((CONV_ROWS, width), lambda s, a: (s, 0)),
        scratch_shapes=[pltpu.VMEM((CONV_ROWS, OFFSETS * channels), jnp.float32)],
    )
    return pl.pallas_call(
        functools.partial(conv_kernel, has_residual=residual is not None),
        grid_spec=grid_spec,
        out_shape=jax.ShapeDtypeStruct((total, width), jnp.bfloat16),
    )(active_rows.reshape(1), *operands)


def pool_kernel(vox_ref, feats_ref, out_ref):
    rows = out_ref.shape[0]
    first = pl.program_id(0) * rows
    summed = None
    for chunk in range(vox_ref.shape[1] // POOL_COLS):
        cols = slice(chunk * POOL_COLS, (chunk + 1) * POOL_COLS)
        ids = first + lax.broadcasted_iota(jnp.int32, (rows, POOL_COLS), 0)
        onehot = (ids == vox_ref[:, cols]).astype(jnp.bfloat16)
        part = jnp.dot(onehot, feats_ref[cols, :], preferred_element_type=jnp.float32)
        summed = part if summed is None else summed + part
    out_ref[...] = summed


def pool(voxel_of_slot, slot_feats, voxel_total):
    slots, width = slot_feats.shape
    return pl.pallas_call(
        pool_kernel,
        grid=(voxel_total // POOL_ROWS,),
        in_specs=[
            pl.BlockSpec((1, slots), lambda v: (0, 0)),
            pl.BlockSpec((slots, width), lambda v: (0, 0)),
        ],
        out_specs=pl.BlockSpec((POOL_ROWS, width), lambda v: (v, 0)),
        out_shape=jax.ShapeDtypeStruct((voxel_total, width), jnp.float32),
    )(voxel_of_slot.reshape(1, slots), slot_feats)


def gather_kernel(index_ref, table_ref, out_ref):
    def pick(i, carry):
        out_ref[pl.ds(i, 1), :] = table_ref[pl.ds(index_ref[i], 1), :]
        return carry

    lax.fori_loop(0, out_ref.shape[0], pick, 0, unroll=64)


def gather_rows(table, index):
    return pl.pallas_call(
        gather_kernel,
        in_specs=[
            pl.BlockSpec(memory_space=pltpu.SMEM),
            pl.BlockSpec(memory_space=pltpu.VMEM),
        ],
        out_specs=pl.BlockSpec(memory_space=pltpu.VMEM),
        out_shape=jax.ShapeDtypeStruct((index.shape[0], table.shape[1]), table.dtype),
    )(index, table)


def per_device(
    point_feats,
    owners,
    voxel_ids,
    active_count,
    halo_blocks,
    neighbors,
    conv1_weight,
    conv1_scale,
    conv1_shift,
    conv2_weight,
    conv2_scale,
    conv2_shift,
    head_weight,
    head_bias,
):
    slab_count = lax.axis_size("slab")
    point_count, in_width = point_feats.shape
    capacity = 3 * point_count // slab_count
    voxel_total = neighbors.shape[2]
    owner_row = owners[0]
    voxel_row = voxel_ids[0]
    owner_hot = (owner_row[:, None] == jnp.arange(slab_count)[None, :]).astype(jnp.bfloat16)
    blocks = owner_hot.reshape(-1, RANK_BLOCK, slab_count)
    before = (
        jnp.arange(RANK_BLOCK)[:, None] > jnp.arange(RANK_BLOCK)[None, :]
    ).astype(jnp.bfloat16)
    within = jnp.einsum("ij,bjk->bik", before, blocks, preferred_element_type=jnp.float32)
    block_totals = jnp.sum(blocks.astype(jnp.float32), axis=1)
    block_starts = jnp.cumsum(block_totals, axis=0) - block_totals
    earlier = (within + block_starts[:, None, :]).reshape(point_count, slab_count)
    ranking = jnp.sum(earlier * owner_hot.astype(jnp.float32), axis=1).astype(jnp.int32)
    slot_number = owner_row * capacity + ranking
    digits = (voxel_row // DIGIT, voxel_row % DIGIT)
    carried = jnp.concatenate(
        [
            point_feats,
            digits[0].astype(jnp.bfloat16)[:, None],
            digits[1].astype(jnp.bfloat16)[:, None],
            jnp.ones((point_count, 1), jnp.bfloat16),
        ],
        axis=1,
    )
    row_width = carried.shape[1]
    send_rows = (
        jnp.zeros((slab_count * capacity, row_width), jnp.bfloat16).at[slot_number].set(carried)
    )
    chunk = capacity * row_width
    dense = -chunk // 128 * -128
    packed = jnp.pad(send_rows.reshape(slab_count, chunk), ((0, 0), (0, dense - chunk)))
    got_packed = lax.all_to_all(
        packed.reshape(slab_count, dense // 128, 128), "slab", 0, 0, tiled=True
    )
    got_rows = got_packed.reshape(slab_count, dense)[:, :chunk].reshape(-1, row_width)
    flat_voxels = (
        got_rows[:, in_width].astype(jnp.int32) * DIGIT
        + got_rows[:, in_width + 1].astype(jnp.int32)
    )
    pooled = pool(flat_voxels, got_rows, voxel_total)
    totals = pooled[:, :in_width]
    counts = pooled[:, in_width + 2]
    voxel_in = (totals / jnp.maximum(counts, 1.0)[:, None]).astype(jnp.bfloat16)
    active_rows = active_count[0, 0] * BLOCK
    halo_list = halo_blocks[0, 0]
    neighbor_table = neighbors[0]
    hidden = convolve(
        extend_rows(voxel_in, halo_list),
        neighbor_table,
        conv1_weight,
        conv1_scale,
        conv1_shift,
        None,
        active_rows,
    )
    refined = convolve(
        extend_rows(hidden, halo_list),
        neighbor_table,
        conv2_weight,
        conv2_scale,
        conv2_shift,
        hidden,
        active_rows,
    )
    voxel_logits = jnp.dot(refined, head_weight, preferred_element_type=jnp.float32) + head_bias
    slot_logits = gather_rows(voxel_logits, flat_voxels).reshape(slab_count, capacity, -1)
    returned = lax.all_to_all(slot_logits, "slab", 0, 0, tiled=True)
    point_logits = gather_rows(returned.reshape(slab_count * capacity, -1), slot_number).T
    summed = all_summed(point_logits, "rot")
    return summed / lax.axis_size("rot")


def solution(mesh):
    return jax.shard_map(
        per_device,
        mesh=mesh,
        in_specs=(
            P("slab", None),
            P("rot", "slab"),
            P("rot", "slab"),
            P("rot", "slab"),
            P("rot", "slab", None, None),
            P("rot", None, "slab"),
            P(),
            P(),
            P(),
            P(),
            P(),
            P(),
            P(),
            P(),
        ),
        out_specs=P(None, "slab"),
        check_vma=False,
    )
```

```python
import functools

import jax
import jax.numpy as jnp
from jax import lax
from jax.experimental import pallas as pl
from jax.experimental.pallas import tpu as pltpu
from jax.sharding import PartitionSpec as P

BLOCK = 128
OFFSETS = 27
CENTRE = 13
UNROLL = 32
CONV_ROWS = 256
POOL_ROWS = 256
POOL_COLS = 512
DIGIT = 64
RANK_BLOCK = 128


def passed_along(shard, axis, by):
    devices = lax.axis_size(axis)
    pairs = [(i, i + by) for i in range(devices) if 0 <= i + by < devices]
    return lax.ppermute(shard, axis, pairs)


def all_summed(values, axis):
    devices = lax.axis_size(axis)
    if devices & (devices - 1):
        return lax.psum(values, axis)
    step = 1
    while step < devices:
        pairs = [(i, i ^ step) for i in range(devices)]
        values = values + lax.ppermute(values, axis, pairs)
        step *= 2
    return values


def extend_rows(features, halo_list):
    channels = features.shape[1]
    block_tiles = features.reshape(-1, BLOCK, channels)
    upward = block_tiles[halo_list[1]].reshape(-1, channels)
    downward = block_tiles[halo_list[0]].reshape(-1, channels)
    from_below = passed_along(upward, "slab", 1)
    from_above = passed_along(downward, "slab", -1)
    rows = features.shape[0] + from_below.shape[0] + from_above.shape[0] + 1
    padding = -rows % 8 + 1
    blank_rows = jnp.zeros((padding, channels), features.dtype)
    extended = jnp.concatenate([features, from_below, from_above, blank_rows], axis=0)
    return extended.astype(jnp.float32)


def conv_kernel(active_ref, nbr_ref, ext_ref, w_ref, scale_ref, shift_ref, *rest, has_residual):
    if has_residual:
        res_ref, out_ref, gathered_ref = rest
    else:
        out_ref, gathered_ref = rest
    rows = out_ref.shape[0]
    channels = ext_ref.shape[1]
    first = pl.multiple_of(pl.program_id(0) * rows, rows)
    active = active_ref[0]

    @pl.when(first < active)
    def _():
        for offset in range(OFFSETS):
            lanes = pl.ds(offset * channels, channels)
            if offset == CENTRE:
                gathered_ref[:, lanes] = ext_ref[pl.ds(first, rows), :]
                continue
            base = offset * rows

            def pick(i, carry):
                row = nbr_ref[base + i]
                gathered_ref[pl.ds(i, 1), lanes] = ext_ref[pl.ds(row, 1), :]
                return carry

            lax.fori_loop(0, rows, pick, 0, unroll=True)
        summed = jnp.dot(
            gathered_ref[...].astype(jnp.bfloat16), w_ref[...], preferred_element_type=jnp.float32
        )
        values = summed * scale_ref[...] + shift_ref[...]
        if has_residual:
            values = values + res_ref[...].astype(jnp.float32)
        living = first + lax.broadcasted_iota(jnp.int32, values.shape, 0) < active
        out_ref[...] = jnp.where(living, jnp.maximum(values, 0.0), 0.0).astype(out_ref.dtype)

    @pl.when(first >= active)
    def _():
        out_ref[...] = jnp.zeros(out_ref.shape, out_ref.dtype)


def convolve(extended, neighbor_table, weight, scale_vec, shift_vec, residual, active_rows):
    total = neighbor_table.shape[1]
    steps = total // CONV_ROWS
    per_step = OFFSETS * CONV_ROWS
    step_block = -per_step // 1024 * -1024
    neighbor_steps = jnp.pad(
        neighbor_table.reshape(OFFSETS, steps, CONV_ROWS).transpose(1, 0, 2).reshape(steps, -1),
        ((0, 0), (0, step_block - per_step)),
    ).reshape(-1)
    ext_rows, width_in = extended.shape
    channels = -width_in // 128 * -128
    width = weight.shape[2]
    extended = jnp.pad(extended, ((0, 0), (0, channels - width_in)))
    weight_flat = jnp.pad(weight, ((0, 0), (0, channels - width_in), (0, 0))).reshape(-1, width)
    in_specs = [
        pl.BlockSpec(
            (step_block,),
            lambda s, a: (s,),
            memory_space=pltpu.SMEM,
            pipeline_mode=pl.Buffered(1),
        ),
        pl.BlockSpec((ext_rows, channels), lambda s, a: (0, 0)),
        pl.BlockSpec(weight_flat.shape, lambda s, a: (0, 0)),
        pl.BlockSpec((1, width), lambda s, a: (0, 0)),
        pl.BlockSpec((1, width), lambda s, a: (0, 0)),
    ]
    operands = [
        neighbor_steps,
        extended,
        weight_flat,
        scale_vec.reshape(1, width),
        shift_vec.reshape(1, width),
    ]
    if residual is not None:
        in_specs.append(pl.BlockSpec((CONV_ROWS, width), lambda s, a: (s, 0)))
        operands.append(residual)
    grid_spec = pltpu.PrefetchScalarGridSpec(
        num_scalar_prefetch=1,
        grid=(steps,),
        in_specs=in_specs,
        out_specs=pl.BlockSpec((CONV_ROWS, width), lambda s, a: (s, 0)),
        scratch_shapes=[pltpu.VMEM((CONV_ROWS, OFFSETS * channels), jnp.float32)],
    )
    return pl.pallas_call(
        functools.partial(conv_kernel, has_residual=residual is not None),
        grid_spec=grid_spec,
        out_shape=jax.ShapeDtypeStruct((total, width), jnp.bfloat16),
    )(active_rows.reshape(1), *operands)


def pool_kernel(vox_ref, feats_ref, out_ref):
    rows = out_ref.shape[0]
    first = pl.program_id(0) * rows
    summed = None
    for chunk in range(vox_ref.shape[1] // POOL_COLS):
        cols = slice(chunk * POOL_COLS, (chunk + 1) * POOL_COLS)
        ids = first + lax.broadcasted_iota(jnp.int32, (rows, POOL_COLS), 0)
        onehot = (ids == vox_ref[:, cols]).astype(jnp.bfloat16)
        part = jnp.dot(onehot, feats_ref[cols, :], preferred_element_type=jnp.float32)
        summed = part if summed is None else summed + part
    out_ref[...] = summed


def pool(voxel_of_slot, slot_feats, voxel_total):
    slots, width = slot_feats.shape
    return pl.pallas_call(
        pool_kernel,
        grid=(voxel_total // POOL_ROWS,),
        in_specs=[
            pl.BlockSpec((1, slots), lambda v: (0, 0)),
            pl.BlockSpec((slots, width), lambda v: (0, 0)),
        ],
        out_specs=pl.BlockSpec((POOL_ROWS, width), lambda v: (v, 0)),
        out_shape=jax.ShapeDtypeStruct((voxel_total, width), jnp.float32),
    )(voxel_of_slot.reshape(1, slots), slot_feats)


def gather_kernel(index_ref, table_ref, out_ref):
    def pick(i, carry):
        out_ref[pl.ds(i, 1), :] = table_ref[pl.ds(index_ref[i], 1), :]
        return carry

    lax.fori_loop(0, out_ref.shape[0], pick, 0, unroll=64)


def gather_rows(table, index):
    return pl.pallas_call(
        gather_kernel,
        in_specs=[
            pl.BlockSpec(memory_space=pltpu.SMEM),
            pl.BlockSpec(memory_space=pltpu.VMEM),
        ],
        out_specs=pl.BlockSpec(memory_space=pltpu.VMEM),
        out_shape=jax.ShapeDtypeStruct((index.shape[0], table.shape[1]), table.dtype),
    )(index, table)


def per_device(
    point_feats,
    owners,
    voxel_ids,
    active_count,
    halo_blocks,
    neighbors,
    conv1_weight,
    conv1_scale,
    conv1_shift,
    conv2_weight,
    conv2_scale,
    conv2_shift,
    head_weight,
    head_bias,
):
    slab_count = lax.axis_size("slab")
    point_count, in_width = point_feats.shape
    capacity = 3 * point_count // slab_count
    voxel_total = neighbors.shape[2]
    owner_row = owners[0]
    voxel_row = voxel_ids[0]
    owner_hot = (owner_row[:, None] == jnp.arange(slab_count)[None, :]).astype(jnp.bfloat16)
    blocks = owner_hot.reshape(-1, RANK_BLOCK, slab_count)
    before = (
        jnp.arange(RANK_BLOCK)[:, None] > jnp.arange(RANK_BLOCK)[None, :]
    ).astype(jnp.bfloat16)
    within = jnp.einsum("ij,bjk->bik", before, blocks, preferred_element_type=jnp.float32)
    block_totals = jnp.sum(blocks.astype(jnp.float32), axis=1)
    block_starts = jnp.cumsum(block_totals, axis=0) - block_totals
    earlier = (within + block_starts[:, None, :]).reshape(point_count, slab_count)
    ranking = jnp.sum(earlier * owner_hot.astype(jnp.float32), axis=1).astype(jnp.int32)
    slot_number = owner_row * capacity + ranking
    digits = (voxel_row // DIGIT, voxel_row % DIGIT)
    carried = jnp.concatenate(
        [
            point_feats,
            digits[0].astype(jnp.bfloat16)[:, None],
            digits[1].astype(jnp.bfloat16)[:, None],
            jnp.ones((point_count, 1), jnp.bfloat16),
        ],
        axis=1,
    )
    row_width = carried.shape[1]
    send_rows = (
        jnp.zeros((slab_count * capacity, row_width), jnp.bfloat16).at[slot_number].set(carried)
    )
    chunk = capacity * row_width
    dense = -chunk // 128 * -128
    packed = jnp.pad(send_rows.reshape(slab_count, chunk), ((0, 0), (0, dense - chunk)))
    got_packed = lax.all_to_all(
        packed.reshape(slab_count, dense // 128, 128), "slab", 0, 0, tiled=True
    )
    got_rows = got_packed.reshape(slab_count, dense)[:, :chunk].reshape(-1, row_width)
    flat_voxels = (
        got_rows[:, in_width].astype(jnp.int32) * DIGIT
        + got_rows[:, in_width + 1].astype(jnp.int32)
    )
    pooled = pool(flat_voxels, got_rows, voxel_total)
    totals = pooled[:, :in_width]
    counts = pooled[:, in_width + 2]
    voxel_in = (totals / jnp.maximum(counts, 1.0)[:, None]).astype(jnp.bfloat16)
    active_rows = active_count[0, 0] * BLOCK
    halo_list = halo_blocks[0, 0]
    neighbor_table = neighbors[0]
    hidden = convolve(
        extend_rows(voxel_in, halo_list),
        neighbor_table,
        conv1_weight,
        conv1_scale,
        conv1_shift,
        None,
        active_rows,
    )
    refined = convolve(
        extend_rows(hidden, halo_list),
        neighbor_table,
        conv2_weight,
        conv2_scale,
        conv2_shift,
        hidden,
        active_rows,
    )
    voxel_logits = jnp.dot(refined, head_weight, preferred_element_type=jnp.float32) + head_bias
    slot_logits = gather_rows(voxel_logits, flat_voxels).reshape(slab_count, capacity, -1)
    returned = lax.all_to_all(slot_logits, "slab", 0, 0, tiled=True)
    point_logits = gather_rows(returned.reshape(slab_count * capacity, -1), slot_number).T
    summed = all_summed(point_logits, "rot")
    return summed / lax.axis_size("rot")


def solution(mesh):
    return jax.shard_map(
        per_device,
        mesh=mesh,
        in_specs=(
            P("slab", None),
            P("rot", "slab"),
            P("rot", "slab"),
            P("rot", "slab"),
            P("rot", "slab", None, None),
            P("rot", None, "slab"),
            P(),
            P(),
            P(),
            P(),
            P(),
            P(),
            P(),
            P(),
        ),
        out_specs=P(None, "slab"),
        check_vma=False,
    )
```

```python
import functools

import jax
import jax.numpy as jnp
from jax import lax
from jax.experimental import pallas as pl
from jax.experimental.pallas import tpu as pltpu
from jax.sharding import PartitionSpec as P

BLOCK = 128
OFFSETS = 27
CENTRE = 13
UNROLL = 32
CONV_ROWS = 256
POOL_ROWS = 256
POOL_COLS = 512
DIGIT = 64
RANK_BLOCK = 128
GATHER_ROWS = 1024


def passed_along(shard, axis, by):
    devices = lax.axis_size(axis)
    pairs = [(i, i + by) for i in range(devices) if 0 <= i + by < devices]
    return lax.ppermute(shard, axis, pairs)


def all_summed(values, axis):
    devices = lax.axis_size(axis)
    if devices & (devices - 1):
        return lax.psum(values, axis)
    step = 1
    while step < devices:
        pairs = [(i, i ^ step) for i in range(devices)]
        values = values + lax.ppermute(values, axis, pairs)
        step *= 2
    return values


def extend_rows(features, halo_list):
    channels = features.shape[1]
    block_tiles = features.reshape(-1, BLOCK, channels)
    upward = block_tiles[halo_list[1]].reshape(-1, channels)
    downward = block_tiles[halo_list[0]].reshape(-1, channels)
    from_below = passed_along(upward, "slab", 1)
    from_above = passed_along(downward, "slab", -1)
    rows = features.shape[0] + from_below.shape[0] + from_above.shape[0] + 1
    padding = -rows % 8 + 1
    blank_rows = jnp.zeros((padding, channels), features.dtype)
    extended = jnp.concatenate([features, from_below, from_above, blank_rows], axis=0)
    return extended.astype(jnp.float32)


def conv_kernel(active_ref, nbr_ref, ext_ref, w_ref, scale_ref, shift_ref, *rest, has_residual):
    if has_residual:
        res_ref, out_ref, gathered_ref = rest
    else:
        out_ref, gathered_ref = rest
    rows = out_ref.shape[0]
    channels = ext_ref.shape[1]
    first = pl.multiple_of(pl.program_id(0) * rows, rows)
    active = active_ref[0]

    @pl.when(first < active)
    def _():
        for offset in range(OFFSETS):
            lanes = pl.ds(offset * channels, channels)
            if offset == CENTRE:
                gathered_ref[:, lanes] = ext_ref[pl.ds(first, rows), :]
                continue
            base = offset * rows

            def pick(i, carry):
                row = nbr_ref[base + i]
                gathered_ref[pl.ds(i, 1), lanes] = ext_ref[pl.ds(row, 1), :]
                return carry

            lax.fori_loop(0, rows, pick, 0, unroll=True)
        summed = jnp.dot(
            gathered_ref[...].astype(jnp.bfloat16), w_ref[...], preferred_element_type=jnp.float32
        )
        values = summed * scale_ref[...] + shift_ref[...]
        if has_residual:
            values = values + res_ref[...].astype(jnp.float32)
        living = first + lax.broadcasted_iota(jnp.int32, values.shape, 0) < active
        out_ref[...] = jnp.where(living, jnp.maximum(values, 0.0), 0.0).astype(out_ref.dtype)

    @pl.when(first >= active)
    def _():
        out_ref[...] = jnp.zeros(out_ref.shape, out_ref.dtype)


def convolve(extended, neighbor_table, weight, scale_vec, shift_vec, residual, active_rows):
    total = neighbor_table.shape[1]
    steps = total // CONV_ROWS
    per_step = OFFSETS * CONV_ROWS
    step_block = -per_step // 1024 * -1024
    neighbor_steps = jnp.pad(
        neighbor_table.reshape(OFFSETS, steps, CONV_ROWS).transpose(1, 0, 2).reshape(steps, -1),
        ((0, 0), (0, step_block - per_step)),
    ).reshape(-1)
    ext_rows, width_in = extended.shape
    channels = -width_in // 128 * -128
    width = weight.shape[2]
    extended = jnp.pad(extended, ((0, 0), (0, channels - width_in)))
    weight_flat = jnp.pad(weight, ((0, 0), (0, channels - width_in), (0, 0))).reshape(-1, width)
    in_specs = [
        pl.BlockSpec(
            (step_block,),
            lambda s, a: (s,),
            memory_space=pltpu.SMEM,
            pipeline_mode=pl.Buffered(1),
        ),
        pl.BlockSpec((ext_rows, channels), lambda s, a: (0, 0)),
        pl.BlockSpec(weight_flat.shape, lambda s, a: (0, 0)),
        pl.BlockSpec((1, width), lambda s, a: (0, 0)),
        pl.BlockSpec((1, width), lambda s, a: (0, 0)),
    ]
    operands = [
        neighbor_steps,
        extended,
        weight_flat,
        scale_vec.reshape(1, width),
        shift_vec.reshape(1, width),
    ]
    if residual is not None:
        in_specs.append(pl.BlockSpec((CONV_ROWS, width), lambda s, a: (s, 0)))
        operands.append(residual)
    grid_spec = pltpu.PrefetchScalarGridSpec(
        num_scalar_prefetch=1,
        grid=(steps,),
        in_specs=in_specs,
        out_specs=pl.BlockSpec((CONV_ROWS, width), lambda s, a: (s, 0)),
        scratch_shapes=[pltpu.VMEM((CONV_ROWS, OFFSETS * channels), jnp.float32)],
    )
    return pl.pallas_call(
        functools.partial(conv_kernel, has_residual=residual is not None),
        grid_spec=grid_spec,
        out_shape=jax.ShapeDtypeStruct((total, width), jnp.bfloat16),
    )(active_rows.reshape(1), *operands)


def pool_kernel(vox_ref, feats_ref, out_ref):
    rows = out_ref.shape[0]
    first = pl.program_id(0) * rows
    summed = None
    for chunk in range(vox_ref.shape[1] // POOL_COLS):
        cols = slice(chunk * POOL_COLS, (chunk + 1) * POOL_COLS)
        ids = first + lax.broadcasted_iota(jnp.int32, (rows, POOL_COLS), 0)
        onehot = (ids == vox_ref[:, cols]).astype(jnp.bfloat16)
        part = jnp.dot(onehot, feats_ref[cols, :], preferred_element_type=jnp.float32)
        summed = part if summed is None else summed + part
    out_ref[...] = summed


def pool(voxel_of_slot, slot_feats, voxel_total):
    slots, width = slot_feats.shape
    return pl.pallas_call(
        pool_kernel,
        grid=(voxel_total // POOL_ROWS,),
        in_specs=[
            pl.BlockSpec((1, slots), lambda v: (0, 0)),
            pl.BlockSpec((slots, width), lambda v: (0, 0)),
        ],
        out_specs=pl.BlockSpec((POOL_ROWS, width), lambda v: (v, 0)),
        out_shape=jax.ShapeDtypeStruct((voxel_total, width), jnp.float32),
    )(voxel_of_slot.reshape(1, slots), slot_feats)


def gather_kernel(index_ref, table_ref, out_ref):
    def pick(i, carry):
        out_ref[pl.ds(i, 1), :] = table_ref[pl.ds(index_ref[i], 1), :]
        return carry

    lax.fori_loop(0, out_ref.shape[0], pick, 0, unroll=True)


def gather_rows(table, index):
    count = index.shape[0]
    rows = GATHER_ROWS if count % GATHER_ROWS == 0 else count
    return pl.pallas_call(
        gather_kernel,
        grid=(count // rows,),
        in_specs=[
            pl.BlockSpec(
                (rows,), lambda s: (s,), memory_space=pltpu.SMEM, pipeline_mode=pl.Buffered(1)
            ),
            pl.BlockSpec(table.shape, lambda s: (0, 0)),
        ],
        out_specs=pl.BlockSpec((rows, table.shape[1]), lambda s: (s, 0)),
        out_shape=jax.ShapeDtypeStruct((count, table.shape[1]), table.dtype),
    )(index, table)


def per_device(
    point_feats,
    owners,
    voxel_ids,
    active_count,
    halo_blocks,
    neighbors,
    conv1_weight,
    conv1_scale,
    conv1_shift,
    conv2_weight,
    conv2_scale,
    conv2_shift,
    head_weight,
    head_bias,
):
    slab_count = lax.axis_size("slab")
    point_count, in_width = point_feats.shape
    capacity = 3 * point_count // slab_count
    voxel_total = neighbors.shape[2]
    owner_row = owners[0]
    voxel_row = voxel_ids[0]
    owner_hot = (owner_row[:, None] == jnp.arange(slab_count)[None, :]).astype(jnp.bfloat16)
    blocks = owner_hot.reshape(-1, RANK_BLOCK, slab_count)
    before = (
        jnp.arange(RANK_BLOCK)[:, None] > jnp.arange(RANK_BLOCK)[None, :]
    ).astype(jnp.bfloat16)
    within = jnp.einsum("ij,bjk->bik", before, blocks, preferred_element_type=jnp.float32)
    block_totals = jnp.sum(blocks.astype(jnp.float32), axis=1)
    block_starts = jnp.cumsum(block_totals, axis=0) - block_totals
    earlier = (within + block_starts[:, None, :]).reshape(point_count, slab_count)
    ranking = jnp.sum(earlier * owner_hot.astype(jnp.float32), axis=1).astype(jnp.int32)
    slot_number = owner_row * capacity + ranking
    digits = (voxel_row // DIGIT, voxel_row % DIGIT)
    carried = jnp.concatenate(
        [
            point_feats,
            digits[0].astype(jnp.bfloat16)[:, None],
            digits[1].astype(jnp.bfloat16)[:, None],
            jnp.ones((point_count, 1), jnp.bfloat16),
        ],
        axis=1,
    )
    row_width = carried.shape[1]
    send_rows = (
        jnp.zeros((slab_count * capacity, row_width), jnp.bfloat16).at[slot_number].set(carried)
    )
    chunk = capacity * row_width
    dense = -chunk // 128 * -128
    packed = jnp.pad(send_rows.reshape(slab_count, chunk), ((0, 0), (0, dense - chunk)))
    got_packed = lax.all_to_all(
        packed.reshape(slab_count, dense // 128, 128), "slab", 0, 0, tiled=True
    )
    got_rows = got_packed.reshape(slab_count, dense)[:, :chunk].reshape(-1, row_width)
    flat_voxels = (
        got_rows[:, in_width].astype(jnp.int32) * DIGIT
        + got_rows[:, in_width + 1].astype(jnp.int32)
    )
    pooled = pool(flat_voxels, got_rows, voxel_total)
    totals = pooled[:, :in_width]
    counts = pooled[:, in_width + 2]
    voxel_in = (totals / jnp.maximum(counts, 1.0)[:, None]).astype(jnp.bfloat16)
    active_rows = active_count[0, 0] * BLOCK
    halo_list = halo_blocks[0, 0]
    neighbor_table = neighbors[0]
    hidden = convolve(
        extend_rows(voxel_in, halo_list),
        neighbor_table,
        conv1_weight,
        conv1_scale,
        conv1_shift,
        None,
        active_rows,
    )
    refined = convolve(
        extend_rows(hidden, halo_list),
        neighbor_table,
        conv2_weight,
        conv2_scale,
        conv2_shift,
        hidden,
        active_rows,
    )
    voxel_logits = jnp.dot(refined, head_weight, preferred_element_type=jnp.float32) + head_bias
    slot_logits = gather_rows(voxel_logits, flat_voxels).reshape(slab_count, capacity, -1)
    returned = lax.all_to_all(slot_logits, "slab", 0, 0, tiled=True)
    point_logits = gather_rows(returned.reshape(slab_count * capacity, -1), slot_number).T
    summed = all_summed(point_logits, "rot")
    return summed / lax.axis_size("rot")


def solution(mesh):
    return jax.shard_map(
        per_device,
        mesh=mesh,
        in_specs=(
            P("slab", None),
            P("rot", "slab"),
            P("rot", "slab"),
            P("rot", "slab"),
            P("rot", "slab", None, None),
            P("rot", None, "slab"),
            P(),
            P(),
            P(),
            P(),
            P(),
            P(),
            P(),
            P(),
        ),
        out_specs=P(None, "slab"),
        check_vma=False,
    )
```

```python
import functools

import jax
import jax.numpy as jnp
from jax import lax
from jax.experimental import pallas as pl
from jax.experimental.pallas import tpu as pltpu
from jax.sharding import PartitionSpec as P

BLOCK = 128
OFFSETS = 27
CENTRE = 13
UNROLL = 32
CONV_ROWS = 256
POOL_ROWS = 256
POOL_COLS = 512
DIGIT = 64
RANK_BLOCK = 128


def passed_along(shard, axis, by):
    devices = lax.axis_size(axis)
    pairs = [(i, i + by) for i in range(devices) if 0 <= i + by < devices]
    return lax.ppermute(shard, axis, pairs)


def all_summed(values, axis):
    devices = lax.axis_size(axis)
    if devices & (devices - 1):
        return lax.psum(values, axis)
    step = 1
    while step < devices:
        pairs = [(i, i ^ step) for i in range(devices)]
        values = values + lax.ppermute(values, axis, pairs)
        step *= 2
    return values


def extend_rows(features, halo_list):
    channels = features.shape[1]
    block_tiles = features.reshape(-1, BLOCK, channels)
    upward = block_tiles[halo_list[1]].reshape(-1, channels)
    downward = block_tiles[halo_list[0]].reshape(-1, channels)
    from_below = passed_along(upward, "slab", 1)
    from_above = passed_along(downward, "slab", -1)
    return features, from_below, from_above


def conv_kernel(
    active_ref, nbr_ref, own_ref, below_ref, above_ref, w_ref, scale_ref, shift_ref, *rest,
    has_residual
):
    if has_residual:
        res_ref, out_ref, gathered_ref, ext_ref = rest
    else:
        out_ref, gathered_ref, ext_ref = rest
    rows = out_ref.shape[0]
    channels = ext_ref.shape[1]
    width_in = own_ref.shape[1]
    first = pl.multiple_of(pl.program_id(0) * rows, rows)
    active = active_ref[0]

    @pl.when(pl.program_id(0) == 0)
    def _():
        own_rows = own_ref.shape[0]
        halo_rows = below_ref.shape[0]
        if width_in != channels:
            ext_ref[...] = jnp.zeros(ext_ref.shape, ext_ref.dtype)
        else:
            tail = own_rows + 2 * halo_rows
            ext_ref[tail:, :] = jnp.zeros((ext_ref.shape[0] - tail, channels), ext_ref.dtype)
        ext_ref[:own_rows, :width_in] = own_ref[...].astype(jnp.float32)
        ext_ref[own_rows : own_rows + halo_rows, :width_in] = below_ref[...].astype(jnp.float32)
        ext_ref[own_rows + halo_rows : own_rows + 2 * halo_rows, :width_in] = above_ref[
            ...
        ].astype(jnp.float32)

    @pl.when(first < active)
    def _():
        for offset in range(OFFSETS):
            lanes = pl.ds(offset * channels, channels)
            if offset == CENTRE:
                gathered_ref[:, lanes] = ext_ref[pl.ds(first, rows), :]
                continue
            base = offset * rows

            def pick(i, carry):
                row = nbr_ref[base + i]
                gathered_ref[pl.ds(i, 1), lanes] = ext_ref[pl.ds(row, 1), :]
                return carry

            lax.fori_loop(0, rows, pick, 0, unroll=True)
        summed = jnp.dot(
            gathered_ref[...].astype(jnp.bfloat16), w_ref[...], preferred_element_type=jnp.float32
        )
        values = summed * scale_ref[...] + shift_ref[...]
        if has_residual:
            values = values + res_ref[...].astype(jnp.float32)
        living = first + lax.broadcasted_iota(jnp.int32, values.shape, 0) < active
        out_ref[...] = jnp.where(living, jnp.maximum(values, 0.0), 0.0).astype(out_ref.dtype)

    @pl.when(first >= active)
    def _():
        out_ref[...] = jnp.zeros(out_ref.shape, out_ref.dtype)


def convolve(pieces, neighbor_table, weight, scale_vec, shift_vec, residual, active_rows):
    total = neighbor_table.shape[1]
    steps = total // CONV_ROWS
    per_step = OFFSETS * CONV_ROWS
    step_block = -per_step // 1024 * -1024
    neighbor_steps = jnp.pad(
        neighbor_table.reshape(OFFSETS, steps, CONV_ROWS).transpose(1, 0, 2).reshape(steps, -1),
        ((0, 0), (0, step_block - per_step)),
    ).reshape(-1)
    own, below, above = pieces
    width_in = own.shape[1]
    ext_rows = -(own.shape[0] + below.shape[0] + above.shape[0] + 1) // 8 * -8
    channels = -width_in // 128 * -128
    width = weight.shape[2]
    weight_flat = jnp.pad(weight, ((0, 0), (0, channels - width_in), (0, 0))).reshape(-1, width)
    in_specs = [
        pl.BlockSpec(
            (step_block,),
            lambda s, a: (s,),
            memory_space=pltpu.SMEM,
            pipeline_mode=pl.Buffered(1),
        ),
        pl.BlockSpec(own.shape, lambda s, a: (0, 0)),
        pl.BlockSpec(below.shape, lambda s, a: (0, 0)),
        pl.BlockSpec(above.shape, lambda s, a: (0, 0)),
        pl.BlockSpec(weight_flat.shape, lambda s, a: (0, 0)),
        pl.BlockSpec((1, width), lambda s, a: (0, 0)),
        pl.BlockSpec((1, width), lambda s, a: (0, 0)),
    ]
    operands = [
        neighbor_steps,
        own,
        below,
        above,
        weight_flat,
        scale_vec.reshape(1, width),
        shift_vec.reshape(1, width),
    ]
    if residual is not None:
        in_specs.append(pl.BlockSpec((CONV_ROWS, width), lambda s, a: (s, 0)))
        operands.append(residual)
    grid_spec = pltpu.PrefetchScalarGridSpec(
        num_scalar_prefetch=1,
        grid=(steps,),
        in_specs=in_specs,
        out_specs=pl.BlockSpec((CONV_ROWS, width), lambda s, a: (s, 0)),
        scratch_shapes=[
            pltpu.VMEM((CONV_ROWS, OFFSETS * channels), jnp.float32),
            pltpu.VMEM((ext_rows, channels), jnp.float32),
        ],
    )
    return pl.pallas_call(
        functools.partial(conv_kernel, has_residual=residual is not None),
        grid_spec=grid_spec,
        out_shape=jax.ShapeDtypeStruct((total, width), jnp.bfloat16),
    )(active_rows.reshape(1), *operands)


def pool_kernel(vox_ref, feats_ref, out_ref):
    rows = out_ref.shape[0]
    first = pl.program_id(0) * rows
    summed = None
    for chunk in range(vox_ref.shape[1] // POOL_COLS):
        cols = slice(chunk * POOL_COLS, (chunk + 1) * POOL_COLS)
        ids = first + lax.broadcasted_iota(jnp.int32, (rows, POOL_COLS), 0)
        onehot = (ids == vox_ref[:, cols]).astype(jnp.bfloat16)
        part = jnp.dot(onehot, feats_ref[cols, :], preferred_element_type=jnp.float32)
        summed = part if summed is None else summed + part
    out_ref[...] = summed


def pool(voxel_of_slot, slot_feats, voxel_total):
    slots, width = slot_feats.shape
    return pl.pallas_call(
        pool_kernel,
        grid=(voxel_total // POOL_ROWS,),
        in_specs=[
            pl.BlockSpec((1, slots), lambda v: (0, 0)),
            pl.BlockSpec((slots, width), lambda v: (0, 0)),
        ],
        out_specs=pl.BlockSpec((POOL_ROWS, width), lambda v: (v, 0)),
        out_shape=jax.ShapeDtypeStruct((voxel_total, width), jnp.float32),
    )(voxel_of_slot.reshape(1, slots), slot_feats)


def gather_kernel(index_ref, table_ref, out_ref):
    def pick(i, carry):
        out_ref[pl.ds(i, 1), :] = table_ref[pl.ds(index_ref[i], 1), :]
        return carry

    lax.fori_loop(0, out_ref.shape[0], pick, 0, unroll=64)


def gather_rows(table, index):
    return pl.pallas_call(
        gather_kernel,
        in_specs=[
            pl.BlockSpec(memory_space=pltpu.SMEM),
            pl.BlockSpec(memory_space=pltpu.VMEM),
        ],
        out_specs=pl.BlockSpec(memory_space=pltpu.VMEM),
        out_shape=jax.ShapeDtypeStruct((index.shape[0], table.shape[1]), table.dtype),
    )(index, table)


def per_device(
    point_feats,
    owners,
    voxel_ids,
    active_count,
    halo_blocks,
    neighbors,
    conv1_weight,
    conv1_scale,
    conv1_shift,
    conv2_weight,
    conv2_scale,
    conv2_shift,
    head_weight,
    head_bias,
):
    slab_count = lax.axis_size("slab")
    point_count, in_width = point_feats.shape
    capacity = 3 * point_count // slab_count
    voxel_total = neighbors.shape[2]
    owner_row = owners[0]
    voxel_row = voxel_ids[0]
    owner_hot = (owner_row[:, None] == jnp.arange(slab_count)[None, :]).astype(jnp.bfloat16)
    blocks = owner_hot.reshape(-1, RANK_BLOCK, slab_count)
    before = (
        jnp.arange(RANK_BLOCK)[:, None] > jnp.arange(RANK_BLOCK)[None, :]
    ).astype(jnp.bfloat16)
    within = jnp.einsum("ij,bjk->bik", before, blocks, preferred_element_type=jnp.float32)
    block_totals = jnp.sum(blocks.astype(jnp.float32), axis=1)
    block_starts = jnp.cumsum(block_totals, axis=0) - block_totals
    earlier = (within + block_starts[:, None, :]).reshape(point_count, slab_count)
    ranking = jnp.sum(earlier * owner_hot.astype(jnp.float32), axis=1).astype(jnp.int32)
    slot_number = owner_row * capacity + ranking
    digits = (voxel_row // DIGIT, voxel_row % DIGIT)
    carried = jnp.concatenate(
        [
            point_feats,
            digits[0].astype(jnp.bfloat16)[:, None],
            digits[1].astype(jnp.bfloat16)[:, None],
            jnp.ones((point_count, 1), jnp.bfloat16),
        ],
        axis=1,
    )
    row_width = carried.shape[1]
    send_rows = (
        jnp.zeros((slab_count * capacity, row_width), jnp.bfloat16).at[slot_number].set(carried)
    )
    chunk = capacity * row_width
    dense = -chunk // 128 * -128
    packed = jnp.pad(send_rows.reshape(slab_count, chunk), ((0, 0), (0, dense - chunk)))
    got_packed = lax.all_to_all(
        packed.reshape(slab_count, dense // 128, 128), "slab", 0, 0, tiled=True
    )
    got_rows = got_packed.reshape(slab_count, dense)[:, :chunk].reshape(-1, row_width)
    flat_voxels = (
        got_rows[:, in_width].astype(jnp.int32) * DIGIT
        + got_rows[:, in_width + 1].astype(jnp.int32)
    )
    pooled = pool(flat_voxels, got_rows, voxel_total)
    totals = pooled[:, :in_width]
    counts = pooled[:, in_width + 2]
    voxel_in = (totals / jnp.maximum(counts, 1.0)[:, None]).astype(jnp.bfloat16)
    active_rows = active_count[0, 0] * BLOCK
    halo_list = halo_blocks[0, 0]
    neighbor_table = neighbors[0]
    hidden = convolve(
        extend_rows(voxel_in, halo_list),
        neighbor_table,
        conv1_weight,
        conv1_scale,
        conv1_shift,
        None,
        active_rows,
    )
    refined = convolve(
        extend_rows(hidden, halo_list),
        neighbor_table,
        conv2_weight,
        conv2_scale,
        conv2_shift,
        hidden,
        active_rows,
    )
    voxel_logits = jnp.dot(refined, head_weight, preferred_element_type=jnp.float32) + head_bias
    slot_logits = gather_rows(voxel_logits, flat_voxels).reshape(slab_count, capacity, -1)
    returned = lax.all_to_all(slot_logits, "slab", 0, 0, tiled=True)
    point_logits = gather_rows(returned.reshape(slab_count * capacity, -1), slot_number).T
    summed = all_summed(point_logits, "rot")
    return summed / lax.axis_size("rot")


def solution(mesh):
    return jax.shard_map(
        per_device,
        mesh=mesh,
        in_specs=(
            P("slab", None),
            P("rot", "slab"),
            P("rot", "slab"),
            P("rot", "slab"),
            P("rot", "slab", None, None),
            P("rot", None, "slab"),
            P(),
            P(),
            P(),
            P(),
            P(),
            P(),
            P(),
            P(),
        ),
        out_specs=P(None, "slab"),
        check_vma=False,
    )
```

```python
import functools

import jax
import jax.numpy as jnp
from jax import lax
from jax.experimental import pallas as pl
from jax.experimental.pallas import tpu as pltpu
from jax.sharding import PartitionSpec as P

BLOCK = 128
OFFSETS = 27
CENTRE = 13
UNROLL = 32
CONV_ROWS = 256
POOL_ROWS = 512
POOL_COLS = 512
DIGIT = 64
RANK_BLOCK = 128


def passed_along(shard, axis, by):
    devices = lax.axis_size(axis)
    pairs = [(i, i + by) for i in range(devices) if 0 <= i + by < devices]
    return lax.ppermute(shard, axis, pairs)


def all_summed(values, axis):
    devices = lax.axis_size(axis)
    if devices & (devices - 1):
        return lax.psum(values, axis)
    step = 1
    while step < devices:
        pairs = [(i, i ^ step) for i in range(devices)]
        values = values + lax.ppermute(values, axis, pairs)
        step *= 2
    return values


def extend_rows(features, halo_list):
    channels = features.shape[1]
    block_tiles = features.reshape(-1, BLOCK, channels)
    upward = block_tiles[halo_list[1]].reshape(-1, channels)
    downward = block_tiles[halo_list[0]].reshape(-1, channels)
    from_below = passed_along(upward, "slab", 1)
    from_above = passed_along(downward, "slab", -1)
    return features, from_below, from_above


def conv_kernel(
    active_ref, nbr_ref, own_ref, below_ref, above_ref, w_ref, scale_ref, shift_ref, *rest,
    has_residual
):
    if has_residual:
        res_ref, out_ref, gathered_ref, ext_ref = rest
    else:
        out_ref, gathered_ref, ext_ref = rest
    rows = out_ref.shape[0]
    channels = ext_ref.shape[1]
    width_in = own_ref.shape[1]
    first = pl.multiple_of(pl.program_id(0) * rows, rows)
    active = active_ref[0]

    @pl.when(pl.program_id(0) == 0)
    def _():
        own_rows = own_ref.shape[0]
        halo_rows = below_ref.shape[0]
        if width_in != channels:
            ext_ref[...] = jnp.zeros(ext_ref.shape, ext_ref.dtype)
        else:
            tail = own_rows + 2 * halo_rows
            ext_ref[tail:, :] = jnp.zeros((ext_ref.shape[0] - tail, channels), ext_ref.dtype)
        ext_ref[:own_rows, :width_in] = own_ref[...].astype(jnp.float32)
        ext_ref[own_rows : own_rows + halo_rows, :width_in] = below_ref[...].astype(jnp.float32)
        ext_ref[own_rows + halo_rows : own_rows + 2 * halo_rows, :width_in] = above_ref[
            ...
        ].astype(jnp.float32)

    @pl.when(first < active)
    def _():
        for offset in range(OFFSETS):
            lanes = pl.ds(offset * channels, channels)
            if offset == CENTRE:
                gathered_ref[:, lanes] = ext_ref[pl.ds(first, rows), :]
                continue
            base = offset * rows

            def pick(i, carry):
                row = nbr_ref[base + i]
                gathered_ref[pl.ds(i, 1), lanes] = ext_ref[pl.ds(row, 1), :]
                return carry

            lax.fori_loop(0, rows, pick, 0, unroll=True)
        summed = jnp.dot(
            gathered_ref[...].astype(jnp.bfloat16), w_ref[...], preferred_element_type=jnp.float32
        )
        values = summed * scale_ref[...] + shift_ref[...]
        if has_residual:
            values = values + res_ref[...].astype(jnp.float32)
        living = first + lax.broadcasted_iota(jnp.int32, values.shape, 0) < active
        out_ref[...] = jnp.where(living, jnp.maximum(values, 0.0), 0.0).astype(out_ref.dtype)

    @pl.when(first >= active)
    def _():
        out_ref[...] = jnp.zeros(out_ref.shape, out_ref.dtype)


def convolve(pieces, neighbor_table, weight, scale_vec, shift_vec, residual, active_rows):
    total = neighbor_table.shape[1]
    steps = total // CONV_ROWS
    per_step = OFFSETS * CONV_ROWS
    step_block = -per_step // 1024 * -1024
    neighbor_steps = jnp.pad(
        neighbor_table.reshape(OFFSETS, steps, CONV_ROWS).transpose(1, 0, 2).reshape(steps, -1),
        ((0, 0), (0, step_block - per_step)),
    ).reshape(-1)
    own, below, above = pieces
    width_in = own.shape[1]
    ext_rows = -(own.shape[0] + below.shape[0] + above.shape[0] + 1) // 8 * -8
    channels = -width_in // 128 * -128
    width = weight.shape[2]
    weight_flat = jnp.pad(weight, ((0, 0), (0, channels - width_in), (0, 0))).reshape(-1, width)
    in_specs = [
        pl.BlockSpec(
            (step_block,),
            lambda s, a: (s,),
            memory_space=pltpu.SMEM,
            pipeline_mode=pl.Buffered(1),
        ),
        pl.BlockSpec(own.shape, lambda s, a: (0, 0)),
        pl.BlockSpec(below.shape, lambda s, a: (0, 0)),
        pl.BlockSpec(above.shape, lambda s, a: (0, 0)),
        pl.BlockSpec(weight_flat.shape, lambda s, a: (0, 0)),
        pl.BlockSpec((1, width), lambda s, a: (0, 0)),
        pl.BlockSpec((1, width), lambda s, a: (0, 0)),
    ]
    operands = [
        neighbor_steps,
        own,
        below,
        above,
        weight_flat,
        scale_vec.reshape(1, width),
        shift_vec.reshape(1, width),
    ]
    if residual is not None:
        in_specs.append(pl.BlockSpec((CONV_ROWS, width), lambda s, a: (s, 0)))
        operands.append(residual)
    grid_spec = pltpu.PrefetchScalarGridSpec(
        num_scalar_prefetch=1,
        grid=(steps,),
        in_specs=in_specs,
        out_specs=pl.BlockSpec((CONV_ROWS, width), lambda s, a: (s, 0)),
        scratch_shapes=[
            pltpu.VMEM((CONV_ROWS, OFFSETS * channels), jnp.float32),
            pltpu.VMEM((ext_rows, channels), jnp.float32),
        ],
    )
    return pl.pallas_call(
        functools.partial(conv_kernel, has_residual=residual is not None),
        grid_spec=grid_spec,
        out_shape=jax.ShapeDtypeStruct((total, width), jnp.bfloat16),
    )(active_rows.reshape(1), *operands)


def pool_kernel(vox_ref, feats_ref, out_ref):
    rows = out_ref.shape[0]
    first = pl.program_id(0) * rows
    summed = None
    for chunk in range(vox_ref.shape[1] // POOL_COLS):
        cols = slice(chunk * POOL_COLS, (chunk + 1) * POOL_COLS)
        ids = first + lax.broadcasted_iota(jnp.int32, (rows, POOL_COLS), 0)
        onehot = (ids == vox_ref[:, cols]).astype(jnp.bfloat16)
        part = jnp.dot(onehot, feats_ref[cols, :], preferred_element_type=jnp.float32)
        summed = part if summed is None else summed + part
    out_ref[...] = summed


def pool(voxel_of_slot, slot_feats, voxel_total):
    slots, width = slot_feats.shape
    return pl.pallas_call(
        pool_kernel,
        grid=(voxel_total // POOL_ROWS,),
        in_specs=[
            pl.BlockSpec((1, slots), lambda v: (0, 0)),
            pl.BlockSpec((slots, width), lambda v: (0, 0)),
        ],
        out_specs=pl.BlockSpec((POOL_ROWS, width), lambda v: (v, 0)),
        out_shape=jax.ShapeDtypeStruct((voxel_total, width), jnp.float32),
    )(voxel_of_slot.reshape(1, slots), slot_feats)


def gather_kernel(index_ref, table_ref, out_ref):
    def pick(i, carry):
        out_ref[pl.ds(i, 1), :] = table_ref[pl.ds(index_ref[i], 1), :]
        return carry

    lax.fori_loop(0, out_ref.shape[0], pick, 0, unroll=64)


def gather_rows(table, index):
    return pl.pallas_call(
        gather_kernel,
        in_specs=[
            pl.BlockSpec(memory_space=pltpu.SMEM),
            pl.BlockSpec(memory_space=pltpu.VMEM),
        ],
        out_specs=pl.BlockSpec(memory_space=pltpu.VMEM),
        out_shape=jax.ShapeDtypeStruct((index.shape[0], table.shape[1]), table.dtype),
    )(index, table)


def per_device(
    point_feats,
    owners,
    voxel_ids,
    active_count,
    halo_blocks,
    neighbors,
    conv1_weight,
    conv1_scale,
    conv1_shift,
    conv2_weight,
    conv2_scale,
    conv2_shift,
    head_weight,
    head_bias,
):
    slab_count = lax.axis_size("slab")
    point_count, in_width = point_feats.shape
    capacity = 3 * point_count // slab_count
    voxel_total = neighbors.shape[2]
    owner_row = owners[0]
    voxel_row = voxel_ids[0]
    owner_hot = (owner_row[:, None] == jnp.arange(slab_count)[None, :]).astype(jnp.bfloat16)
    blocks = owner_hot.reshape(-1, RANK_BLOCK, slab_count)
    before = (
        jnp.arange(RANK_BLOCK)[:, None] > jnp.arange(RANK_BLOCK)[None, :]
    ).astype(jnp.bfloat16)
    within = jnp.einsum("ij,bjk->bik", before, blocks, preferred_element_type=jnp.float32)
    block_totals = jnp.sum(blocks.astype(jnp.float32), axis=1)
    block_starts = jnp.cumsum(block_totals, axis=0) - block_totals
    earlier = (within + block_starts[:, None, :]).reshape(point_count, slab_count)
    ranking = jnp.sum(earlier * owner_hot.astype(jnp.float32), axis=1).astype(jnp.int32)
    slot_number = owner_row * capacity + ranking
    digits = (voxel_row // DIGIT, voxel_row % DIGIT)
    carried = jnp.concatenate(
        [
            point_feats,
            digits[0].astype(jnp.bfloat16)[:, None],
            digits[1].astype(jnp.bfloat16)[:, None],
            jnp.ones((point_count, 1), jnp.bfloat16),
        ],
        axis=1,
    )
    row_width = carried.shape[1]
    send_rows = (
        jnp.zeros((slab_count * capacity, row_width), jnp.bfloat16).at[slot_number].set(carried)
    )
    chunk = capacity * row_width
    dense = -chunk // 128 * -128
    packed = jnp.pad(send_rows.reshape(slab_count, chunk), ((0, 0), (0, dense - chunk)))
    got_packed = lax.all_to_all(
        packed.reshape(slab_count, dense // 128, 128), "slab", 0, 0, tiled=True
    )
    got_rows = got_packed.reshape(slab_count, dense)[:, :chunk].reshape(-1, row_width)
    flat_voxels = (
        got_rows[:, in_width].astype(jnp.int32) * DIGIT
        + got_rows[:, in_width + 1].astype(jnp.int32)
    )
    pooled = pool(flat_voxels, got_rows, voxel_total)
    totals = pooled[:, :in_width]
    counts = pooled[:, in_width + 2]
    voxel_in = (totals / jnp.maximum(counts, 1.0)[:, None]).astype(jnp.bfloat16)
    active_rows = active_count[0, 0] * BLOCK
    halo_list = halo_blocks[0, 0]
    neighbor_table = neighbors[0]
    hidden = convolve(
        extend_rows(voxel_in, halo_list),
        neighbor_table,
        conv1_weight,
        conv1_scale,
        conv1_shift,
        None,
        active_rows,
    )
    refined = convolve(
        extend_rows(hidden, halo_list),
        neighbor_table,
        conv2_weight,
        conv2_scale,
        conv2_shift,
        hidden,
        active_rows,
    )
    voxel_logits = jnp.dot(refined, head_weight, preferred_element_type=jnp.float32) + head_bias
    slot_logits = gather_rows(voxel_logits, flat_voxels).reshape(slab_count, capacity, -1)
    returned = lax.all_to_all(slot_logits, "slab", 0, 0, tiled=True)
    point_logits = gather_rows(returned.reshape(slab_count * capacity, -1), slot_number).T
    summed = all_summed(point_logits, "rot")
    return summed / lax.axis_size("rot")


def solution(mesh):
    return jax.shard_map(
        per_device,
        mesh=mesh,
        in_specs=(
            P("slab", None),
            P("rot", "slab"),
            P("rot", "slab"),
            P("rot", "slab"),
            P("rot", "slab", None, None),
            P("rot", None, "slab"),
            P(),
            P(),
            P(),
            P(),
            P(),
            P(),
            P(),
            P(),
        ),
        out_specs=P(None, "slab"),
        check_vma=False,
    )
```

```python
import functools

import jax
import jax.numpy as jnp
from jax import lax
from jax.experimental import pallas as pl
from jax.experimental.pallas import tpu as pltpu
from jax.sharding import PartitionSpec as P

BLOCK = 128
OFFSETS = 27
CENTRE = 13
UNROLL = 32
CONV_ROWS = 256
POOL_ROWS = 1024
POOL_COLS = 512
DIGIT = 64
RANK_BLOCK = 128


def passed_along(shard, axis, by):
    devices = lax.axis_size(axis)
    pairs = [(i, i + by) for i in range(devices) if 0 <= i + by < devices]
    return lax.ppermute(shard, axis, pairs)


def all_summed(values, axis):
    devices = lax.axis_size(axis)
    if devices & (devices - 1):
        return lax.psum(values, axis)
    step = 1
    while step < devices:
        pairs = [(i, i ^ step) for i in range(devices)]
        values = values + lax.ppermute(values, axis, pairs)
        step *= 2
    return values


def extend_rows(features, halo_list):
    channels = features.shape[1]
    block_tiles = features.reshape(-1, BLOCK, channels)
    upward = block_tiles[halo_list[1]].reshape(-1, channels)
    downward = block_tiles[halo_list[0]].reshape(-1, channels)
    from_below = passed_along(upward, "slab", 1)
    from_above = passed_along(downward, "slab", -1)
    return features, from_below, from_above


def conv_kernel(
    active_ref, nbr_ref, own_ref, below_ref, above_ref, w_ref, scale_ref, shift_ref, *rest,
    has_residual
):
    if has_residual:
        res_ref, out_ref, gathered_ref, ext_ref = rest
    else:
        out_ref, gathered_ref, ext_ref = rest
    rows = out_ref.shape[0]
    channels = ext_ref.shape[1]
    width_in = own_ref.shape[1]
    first = pl.multiple_of(pl.program_id(0) * rows, rows)
    active = active_ref[0]

    @pl.when(pl.program_id(0) == 0)
    def _():
        own_rows = own_ref.shape[0]
        halo_rows = below_ref.shape[0]
        if width_in != channels:
            ext_ref[...] = jnp.zeros(ext_ref.shape, ext_ref.dtype)
        else:
            tail = own_rows + 2 * halo_rows
            ext_ref[tail:, :] = jnp.zeros((ext_ref.shape[0] - tail, channels), ext_ref.dtype)
        ext_ref[:own_rows, :width_in] = own_ref[...].astype(jnp.float32)
        ext_ref[own_rows : own_rows + halo_rows, :width_in] = below_ref[...].astype(jnp.float32)
        ext_ref[own_rows + halo_rows : own_rows + 2 * halo_rows, :width_in] = above_ref[
            ...
        ].astype(jnp.float32)

    @pl.when(first < active)
    def _():
        for offset in range(OFFSETS):
            lanes = pl.ds(offset * channels, channels)
            if offset == CENTRE:
                gathered_ref[:, lanes] = ext_ref[pl.ds(first, rows), :]
                continue
            base = offset * rows

            def pick(i, carry):
                row = nbr_ref[base + i]
                gathered_ref[pl.ds(i, 1), lanes] = ext_ref[pl.ds(row, 1), :]
                return carry

            lax.fori_loop(0, rows, pick, 0, unroll=True)
        summed = jnp.dot(
            gathered_ref[...].astype(jnp.bfloat16), w_ref[...], preferred_element_type=jnp.float32
        )
        values = summed * scale_ref[...] + shift_ref[...]
        if has_residual:
            values = values + res_ref[...].astype(jnp.float32)
        living = first + lax.broadcasted_iota(jnp.int32, values.shape, 0) < active
        out_ref[...] = jnp.where(living, jnp.maximum(values, 0.0), 0.0).astype(out_ref.dtype)

    @pl.when(first >= active)
    def _():
        out_ref[...] = jnp.zeros(out_ref.shape, out_ref.dtype)


def convolve(pieces, neighbor_table, weight, scale_vec, shift_vec, residual, active_rows):
    total = neighbor_table.shape[1]
    steps = total // CONV_ROWS
    per_step = OFFSETS * CONV_ROWS
    step_block = -per_step // 1024 * -1024
    neighbor_steps = jnp.pad(
        neighbor_table.reshape(OFFSETS, steps, CONV_ROWS).transpose(1, 0, 2).reshape(steps, -1),
        ((0, 0), (0, step_block - per_step)),
    ).reshape(-1)
    own, below, above = pieces
    width_in = own.shape[1]
    ext_rows = -(own.shape[0] + below.shape[0] + above.shape[0] + 1) // 8 * -8
    channels = -width_in // 128 * -128
    width = weight.shape[2]
    weight_flat = jnp.pad(weight, ((0, 0), (0, channels - width_in), (0, 0))).reshape(-1, width)
    in_specs = [
        pl.BlockSpec(
            (step_block,),
            lambda s, a: (s,),
            memory_space=pltpu.SMEM,
            pipeline_mode=pl.Buffered(1),
        ),
        pl.BlockSpec(own.shape, lambda s, a: (0, 0)),
        pl.BlockSpec(below.shape, lambda s, a: (0, 0)),
        pl.BlockSpec(above.shape, lambda s, a: (0, 0)),
        pl.BlockSpec(weight_flat.shape, lambda s, a: (0, 0)),
        pl.BlockSpec((1, width), lambda s, a: (0, 0)),
        pl.BlockSpec((1, width), lambda s, a: (0, 0)),
    ]
    operands = [
        neighbor_steps,
        own,
        below,
        above,
        weight_flat,
        scale_vec.reshape(1, width),
        shift_vec.reshape(1, width),
    ]
    if residual is not None:
        in_specs.append(pl.BlockSpec((CONV_ROWS, width), lambda s, a: (s, 0)))
        operands.append(residual)
    grid_spec = pltpu.PrefetchScalarGridSpec(
        num_scalar_prefetch=1,
        grid=(steps,),
        in_specs=in_specs,
        out_specs=pl.BlockSpec((CONV_ROWS, width), lambda s, a: (s, 0)),
        scratch_shapes=[
            pltpu.VMEM((CONV_ROWS, OFFSETS * channels), jnp.float32),
            pltpu.VMEM((ext_rows, channels), jnp.float32),
        ],
    )
    return pl.pallas_call(
        functools.partial(conv_kernel, has_residual=residual is not None),
        grid_spec=grid_spec,
        out_shape=jax.ShapeDtypeStruct((total, width), jnp.bfloat16),
    )(active_rows.reshape(1), *operands)


def pool_kernel(vox_ref, feats_ref, out_ref):
    rows = out_ref.shape[0]
    first = pl.program_id(0) * rows
    summed = None
    for chunk in range(vox_ref.shape[1] // POOL_COLS):
        cols = slice(chunk * POOL_COLS, (chunk + 1) * POOL_COLS)
        ids = first + lax.broadcasted_iota(jnp.int32, (rows, POOL_COLS), 0)
        onehot = (ids == vox_ref[:, cols]).astype(jnp.bfloat16)
        part = jnp.dot(onehot, feats_ref[cols, :], preferred_element_type=jnp.float32)
        summed = part if summed is None else summed + part
    out_ref[...] = summed


def pool(voxel_of_slot, slot_feats, voxel_total):
    slots, width = slot_feats.shape
    return pl.pallas_call(
        pool_kernel,
        grid=(voxel_total // POOL_ROWS,),
        in_specs=[
            pl.BlockSpec((1, slots), lambda v: (0, 0)),
            pl.BlockSpec((slots, width), lambda v: (0, 0)),
        ],
        out_specs=pl.BlockSpec((POOL_ROWS, width), lambda v: (v, 0)),
        out_shape=jax.ShapeDtypeStruct((voxel_total, width), jnp.float32),
    )(voxel_of_slot.reshape(1, slots), slot_feats)


def gather_kernel(index_ref, table_ref, out_ref):
    def pick(i, carry):
        out_ref[pl.ds(i, 1), :] = table_ref[pl.ds(index_ref[i], 1), :]
        return carry

    lax.fori_loop(0, out_ref.shape[0], pick, 0, unroll=64)


def gather_rows(table, index):
    return pl.pallas_call(
        gather_kernel,
        in_specs=[
            pl.BlockSpec(memory_space=pltpu.SMEM),
            pl.BlockSpec(memory_space=pltpu.VMEM),
        ],
        out_specs=pl.BlockSpec(memory_space=pltpu.VMEM),
        out_shape=jax.ShapeDtypeStruct((index.shape[0], table.shape[1]), table.dtype),
    )(index, table)


def per_device(
    point_feats,
    owners,
    voxel_ids,
    active_count,
    halo_blocks,
    neighbors,
    conv1_weight,
    conv1_scale,
    conv1_shift,
    conv2_weight,
    conv2_scale,
    conv2_shift,
    head_weight,
    head_bias,
):
    slab_count = lax.axis_size("slab")
    point_count, in_width = point_feats.shape
    capacity = 3 * point_count // slab_count
    voxel_total = neighbors.shape[2]
    owner_row = owners[0]
    voxel_row = voxel_ids[0]
    owner_hot = (owner_row[:, None] == jnp.arange(slab_count)[None, :]).astype(jnp.bfloat16)
    blocks = owner_hot.reshape(-1, RANK_BLOCK, slab_count)
    before = (
        jnp.arange(RANK_BLOCK)[:, None] > jnp.arange(RANK_BLOCK)[None, :]
    ).astype(jnp.bfloat16)
    within = jnp.einsum("ij,bjk->bik", before, blocks, preferred_element_type=jnp.float32)
    block_totals = jnp.sum(blocks.astype(jnp.float32), axis=1)
    block_starts = jnp.cumsum(block_totals, axis=0) - block_totals
    earlier = (within + block_starts[:, None, :]).reshape(point_count, slab_count)
    ranking = jnp.sum(earlier * owner_hot.astype(jnp.float32), axis=1).astype(jnp.int32)
    slot_number = owner_row * capacity + ranking
    digits = (voxel_row // DIGIT, voxel_row % DIGIT)
    carried = jnp.concatenate(
        [
            point_feats,
            digits[0].astype(jnp.bfloat16)[:, None],
            digits[1].astype(jnp.bfloat16)[:, None],
            jnp.ones((point_count, 1), jnp.bfloat16),
        ],
        axis=1,
    )
    row_width = carried.shape[1]
    send_rows = (
        jnp.zeros((slab_count * capacity, row_width), jnp.bfloat16).at[slot_number].set(carried)
    )
    chunk = capacity * row_width
    dense = -chunk // 128 * -128
    packed = jnp.pad(send_rows.reshape(slab_count, chunk), ((0, 0), (0, dense - chunk)))
    got_packed = lax.all_to_all(
        packed.reshape(slab_count, dense // 128, 128), "slab", 0, 0, tiled=True
    )
    got_rows = got_packed.reshape(slab_count, dense)[:, :chunk].reshape(-1, row_width)
    flat_voxels = (
        got_rows[:, in_width].astype(jnp.int32) * DIGIT
        + got_rows[:, in_width + 1].astype(jnp.int32)
    )
    pooled = pool(flat_voxels, got_rows, voxel_total)
    totals = pooled[:, :in_width]
    counts = pooled[:, in_width + 2]
    voxel_in = (totals / jnp.maximum(counts, 1.0)[:, None]).astype(jnp.bfloat16)
    active_rows = active_count[0, 0] * BLOCK
    halo_list = halo_blocks[0, 0]
    neighbor_table = neighbors[0]
    hidden = convolve(
        extend_rows(voxel_in, halo_list),
        neighbor_table,
        conv1_weight,
        conv1_scale,
        conv1_shift,
        None,
        active_rows,
    )
    refined = convolve(
        extend_rows(hidden, halo_list),
        neighbor_table,
        conv2_weight,
        conv2_scale,
        conv2_shift,
        hidden,
        active_rows,
    )
    voxel_logits = jnp.dot(refined, head_weight, preferred_element_type=jnp.float32) + head_bias
    slot_logits = gather_rows(voxel_logits, flat_voxels).reshape(slab_count, capacity, -1)
    returned = lax.all_to_all(slot_logits, "slab", 0, 0, tiled=True)
    point_logits = gather_rows(returned.reshape(slab_count * capacity, -1), slot_number).T
    summed = all_summed(point_logits, "rot")
    return summed / lax.axis_size("rot")


def solution(mesh):
    return jax.shard_map(
        per_device,
        mesh=mesh,
        in_specs=(
            P("slab", None),
            P("rot", "slab"),
            P("rot", "slab"),
            P("rot", "slab"),
            P("rot", "slab", None, None),
            P("rot", None, "slab"),
            P(),
            P(),
            P(),
            P(),
            P(),
            P(),
            P(),
            P(),
        ),
        out_specs=P(None, "slab"),
        check_vma=False,
    )
```
